1024 devices in a mesh: seq: 128 (over y_hi, z, core), head: 8 (over y_lo, x).
Axes of the slice: x: 4, y: 8 (y_hi: 4, y_lo: 2; y = y_hi * 2 + y_lo), z: 16, core: 2. Of those that a mesh axis runs over, the one named last changes fastest.
Arguments:
- teacher_query: bfloat16 [16384, 2048], P('seq', 'head'), may hold values from -98 to 98
- teacher_key: bfloat16 [16384, 2048], P('seq', 'head'), may hold values from -98 to 98
- teacher_value: bfloat16 [16384, 2048], P('seq', 'head'), may hold values from -6 to 6
- student_query: bfloat16 [16384, 2048], P('seq', 'head'), may hold values from -80 to 80
- student_key: bfloat16 [16384, 2048], P('seq', 'head'), may hold values from -80 to 80
- student_value: bfloat16 [16384, 2048], P('seq', 'head'), may hold values from -6 to 6
- segment_ids: int32 [16384], P('seq'), may hold values from 0 to 7, never falling along the last dimension, each value on 1 to 4096 neighbouring positions
- language_ids: int32 [16384], P('seq'), may hold values from 0 to 15
- language_weight: float32 [16], replicated, may hold values from 1 to 16
- teacher_out_proj: bfloat16 [4608, 2048], P('head'), may hold values from -0.125 to 0.125
- student_out_proj: bfloat16 [2048, 2304], P('head'), may hold values from -0.125 to 0.125
- match_proj: bfloat16 [4608, 2304], P('head'), may hold values from -0.09375 to 0.09375
Outputs:
- grad_query: float32 [16384, 2048], P('seq', 'head')
- grad_key: float32 [16384, 2048], P('seq', 'head')
- grad_value: float32 [16384, 2048], P('seq', 'head')
The draws below stay inside these ranges and needn't reach their ends.
All inputs are finite; a program needn't handle non-finite values.
Results may differ from the reference program's by a relative error of at most 0.02.
Values may be sent and summed in bfloat16 or wider, within the bound.
No kernel may reach another device: no remote copies, remote signals or barrier semaphores. Data moves between devices by JAX's collectives and lax.ppermute only.
A program may use at most 64 MiB of HBM per device.

```python
import math
import jax
import jax.numpy as jnp
import numpy as np
from jax import lax

D_T = 4608
HEADS_T = 16
DH_T = 128
D_S = 2304
HEADS_S = 8
DH_S = 256
WINDOW = 1024
LANGS = 16
TOKENS = 16384
DOCS = 8
DOC_MOST = 4096


teacher_scale = 144.0 ** (-0.5)


def aligned_pair(key, heads, depth, scale):
    shape = (TOKENS, heads * depth)
    query = jnp.clip(jax.random.normal(jax.random.fold_in(key, 1), shape, jnp.float32), -6.0, 6.0)
    keys_drawn = jnp.clip(jax.random.normal(jax.random.fold_in(key, 2), shape, jnp.float32), -6.0, 6.0)
    return (query, keys_drawn)


def draw_teacher_query(key, part):
    return aligned_pair(jax.random.fold_in(key, 11), HEADS_T, DH_T, teacher_scale)[0].astype(jnp.bfloat16)


def draw_teacher_key(key, part):
    return aligned_pair(jax.random.fold_in(key, 11), HEADS_T, DH_T, teacher_scale)[1].astype(jnp.bfloat16)


def draw_student_query(key, part):
    return aligned_pair(jax.random.fold_in(key, 23), HEADS_S, DH_S, DH_S ** (-0.5))[0].astype(jnp.bfloat16)


def draw_student_key(key, part):
    return aligned_pair(jax.random.fold_in(key, 23), HEADS_S, DH_S, DH_S ** (-0.5))[1].astype(jnp.bfloat16)


def set_ends(result, rng, smallest, largest):
    index_at = [jax.random.randint(jax.random.fold_in(rng, axis), (), 0, length) for axis, length in enumerate(result.shape)]
    longest = result.shape.index(max(result.shape))
    neighbour = index_at[:longest] + [(index_at[longest] + 1) % result.shape[longest]] + index_at[longest + 1:]
    return result.at[tuple(index_at)].set(smallest).at[tuple(neighbour)].set(largest)


def steps_of(stream_key, extent, shards, low, top_value):
    loudness = 1.0
    for position, blocks in shards:
        heights = jax.random.uniform(jax.random.fold_in(jax.random.fold_in(stream_key, 6), position), (blocks,), jnp.float32, low / len(shards), top_value / len(shards))
        loudness = loudness * jnp.repeat(jnp.exp(heights), extent[position] // blocks).reshape((-1,) + (1,) * (len(extent) - 1 - position))
    return loudness


def length_profile(amount, total, most, lean):
    loads = [(1 << 20) // math.isqrt(rank ** lean) + 1 for rank in range(2, amount + 1)]
    spare, holding = total - most - (amount - 1), [1] * (amount - 1)
    while spare > 0:
        candidates = [i for i in range(amount - 1) if holding[i] < most]
        whole, budget = sum([loads[i] for i in candidates]), spare
        for i in candidates:
            addition = min(most - holding[i], max(1, budget * loads[i] // whole), spare)
            holding[i] = holding[i] + addition
            spare = spare - addition
    return np.array([most] + holding)


def uneven(stream_key, amount, total, limit, skew):
    if amount == 2:
        one = jax.random.randint(stream_key, (), max(1, total - limit), min(limit, total - 1) + 1)
        return jnp.stack([one, total - one])
    lengths = jnp.asarray(length_profile(amount, total, limit, skew), jnp.int32)
    twos = (amount - 1) // 2
    giver, sink = lengths[1:1 + 2 * twos:2], lengths[2:2 + 2 * twos:2]
    room = jnp.minimum(giver - 1, limit - sink)
    passed = jax.random.randint(jax.random.fold_in(stream_key, 1), (twos,), 0, 1 << 20) % (room + 1)
    lengths = lengths.at[1:1 + 2 * twos:2].set(giver - passed).at[2:2 + 2 * twos:2].set(sink + passed)
    return lengths[jax.random.permutation(jax.random.fold_in(stream_key, 2), amount)]


def scatter_about(key, dims, deviation, limit, cuts=(), held_as=jnp.bfloat16):
    loudness = steps_of(key, dims, cuts, -0.22, 0.18) if cuts else 1.0
    values = jax.random.normal(key, dims, jnp.float32) * deviation * loudness
    return jnp.minimum(jnp.maximum(values, -limit), limit).astype(held_as)


def setup_inputs(seed: int = 0) -> dict:
    seeds = jax.random.split(jax.random.key(seed), 13)
    return {
        "teacher_query": draw_teacher_query(jax.random.fold_in(seeds[12], 71), 0),
        "teacher_key": draw_teacher_key(jax.random.fold_in(seeds[12], 71), 0),
        "teacher_value": scatter_about(seeds[2], (TOKENS, HEADS_T * DH_T), 1.0, 6.0, ((0, 128), (1, 8))),
        "student_query": draw_student_query(jax.random.fold_in(seeds[12], 71), 0),
        "student_key": draw_student_key(jax.random.fold_in(seeds[12], 71), 0),
        "student_value": scatter_about(seeds[5], (TOKENS, HEADS_S * DH_S), 1.0, 6.0, ((0, 128), (1, 8))),
        "segment_ids": jnp.searchsorted(jnp.cumsum(uneven(seeds[6], DOCS, TOKENS, DOC_MOST, 0)), jnp.arange(TOKENS), side="right").astype(jnp.int32),
        "language_ids": set_ends(jax.random.randint(seeds[7], (TOKENS,), 0, LANGS), jax.random.fold_in(seeds[7], 1), 0, LANGS - 1).astype(jnp.int32),
        "language_weight": jnp.clip(jnp.exp(jax.random.uniform(seeds[8], (LANGS,), jnp.float32, math.log(1.0), math.log(16.0))), 1.0, 16.0),
        "teacher_out_proj": scatter_about(seeds[9], (D_T, HEADS_T * DH_T), (HEADS_T * DH_T) ** -0.5, 0.125, ((0, 8),)),
        "student_out_proj": scatter_about(seeds[10], (HEADS_S * DH_S, D_S), (HEADS_S * DH_S) ** -0.5, 0.125, ((0, 8),)),
        "match_proj": scatter_about(seeds[11], (D_T, D_S), D_T ** -0.5, 0.09375, ((0, 8),)),
    }


teacher_scale = 144.0 ** -0.5
negative = -1.0e30


def round_half(values):
    return lax.optimization_barrier(values.astype(jnp.bfloat16)).astype(jnp.float32)


def padded_inputs(query, key, value, segments, heads, depth):
    total = query.shape[0]
    query_three = query.reshape(total, heads, depth)
    key_pad = jnp.concatenate([jnp.zeros((WINDOW, heads, depth), key.dtype), key.reshape(total, heads, depth)], 0)
    value_pad = jnp.concatenate([jnp.zeros((WINDOW, heads, depth), value.dtype), value.reshape(total, heads, depth)], 0)
    marks_pad = jnp.concatenate([jnp.full((WINDOW,), -1, jnp.int32), segments.astype(jnp.int32)], 0)
    return query_three, key_pad, value_pad, marks_pad


def block_probs(query_three, key_pad, segments, marks_pad, start, block_rows, scale):
    query_part = lax.dynamic_slice_in_dim(query_three, start, block_rows, 0).astype(jnp.float32)
    key_part = lax.dynamic_slice_in_dim(key_pad, start, block_rows + WINDOW, 0).astype(jnp.float32)
    scores = jnp.einsum("qhd,khd->hqk", query_part, key_part) * scale
    positions_q = start + jnp.arange(block_rows, dtype=jnp.int32)
    positions_k = start - WINDOW + jnp.arange(block_rows + WINDOW, dtype=jnp.int32)
    distance = positions_q[:, None] - positions_k[None, :]
    marks_q = lax.dynamic_slice_in_dim(segments.astype(jnp.int32), start, block_rows, 0)
    marks_k = lax.dynamic_slice_in_dim(marks_pad, start, block_rows + WINDOW, 0)
    allowed = (marks_q[:, None] == marks_k[None, :]) & (distance >= 0) & (distance < WINDOW)
    highest = jnp.max(jnp.where(allowed[None], scores, negative), axis=-1, keepdims=True)
    weights = jnp.where(allowed[None], jnp.exp(scores - highest), 0.0)
    probability = weights / jnp.sum(weights, axis=-1, keepdims=True)
    return probability, query_part, key_part


def forward_layer(query, key, value, segments, heads, depth, scale):
    total = query.shape[0]
    block_rows = min(512, total)
    count_blocks = total // block_rows
    query_three, key_pad, value_pad, marks_pad = padded_inputs(query, key, value, segments, heads, depth)

    def one_block(number):
        start = number * block_rows
        probability, query_part, key_part = block_probs(query_three, key_pad, segments, marks_pad, start, block_rows, scale)
        value_part = lax.dynamic_slice_in_dim(value_pad, start, block_rows + WINDOW, 0).astype(jnp.float32)
        mixed = jnp.einsum("hqk,khd->qhd", round_half(probability), value_part)
        return mixed.astype(jnp.bfloat16)

    blocks = lax.map(one_block, jnp.arange(count_blocks, dtype=jnp.int32))
    return blocks.reshape(total, heads * depth)


def backward_layer(query, key, value, segments, grad_heads, heads, depth, scale):
    total = query.shape[0]
    block_rows = min(512, total)
    count_blocks = total // block_rows
    query_three, key_pad, value_pad, marks_pad = padded_inputs(query, key, value, segments, heads, depth)
    grad_three = grad_heads.reshape(total, heads, depth)

    def one_step(carried, number):
        key_acc, value_acc = carried
        start = number * block_rows
        probability, query_part, key_part = block_probs(query_three, key_pad, segments, marks_pad, start, block_rows, scale)
        value_part = lax.dynamic_slice_in_dim(value_pad, start, block_rows + WINDOW, 0).astype(jnp.float32)
        grad_part = lax.dynamic_slice_in_dim(grad_three, start, block_rows, 0).astype(jnp.float32)
        grad_probs = jnp.einsum("qhd,khd->hqk", grad_part, value_part)
        inner = jnp.sum(probability * grad_probs, axis=-1, keepdims=True)
        grad_scores = round_half(probability * (grad_probs - inner))
        grad_q = scale * jnp.einsum("hqk,khd->qhd", grad_scores, key_part)
        grad_k = scale * jnp.einsum("hqk,qhd->khd", grad_scores, query_part)
        grad_v = jnp.einsum("hqk,qhd->khd", round_half(probability), grad_part)
        key_old = lax.dynamic_slice_in_dim(key_acc, start, block_rows + WINDOW, 0)
        value_old = lax.dynamic_slice_in_dim(value_acc, start, block_rows + WINDOW, 0)
        key_acc = lax.dynamic_update_slice_in_dim(key_acc, key_old + grad_k, start, 0)
        value_acc = lax.dynamic_update_slice_in_dim(value_acc, value_old + grad_v, start, 0)
        return (key_acc, value_acc), grad_q

    empty = jnp.zeros((total + WINDOW, heads, depth), jnp.float32)
    (key_acc, value_acc), grad_blocks = lax.scan(one_step, (empty, empty), jnp.arange(count_blocks, dtype=jnp.int32))
    grad_query = grad_blocks.reshape(total, heads * depth)
    grad_key = key_acc[WINDOW:].reshape(total, heads * depth)
    grad_value = value_acc[WINDOW:].reshape(total, heads * depth)
    return grad_query, grad_key, grad_value


def reference(teacher_query, teacher_key, teacher_value, student_query, student_key, student_value, segment_ids, language_ids, language_weight, teacher_out_proj, student_out_proj, match_proj):
    teacher_mix = forward_layer(teacher_query, teacher_key, teacher_value, segment_ids, HEADS_T, DH_T, teacher_scale)
    target = jnp.dot(teacher_mix, teacher_out_proj.T, preferred_element_type=jnp.float32).astype(jnp.bfloat16)
    student_scale = DH_S ** -0.5
    student_mix = forward_layer(student_query, student_key, student_value, segment_ids, HEADS_S, DH_S, student_scale)
    residual = jnp.dot(student_mix, student_out_proj, preferred_element_type=jnp.float32) - jnp.dot(target, match_proj, preferred_element_type=jnp.float32)
    lang_table = jnp.arange(LANGS, dtype=jnp.int32)
    token_weight = jnp.sum(jnp.where(language_ids[:, None] == lang_table[None, :], language_weight[None, :], 0.0), axis=1)
    grad_mix = (token_weight[:, None] * residual).astype(jnp.bfloat16)
    grad_heads = jnp.dot(grad_mix, student_out_proj.T, preferred_element_type=jnp.float32).astype(jnp.bfloat16)
    grad_query, grad_key, grad_value = backward_layer(student_query, student_key, student_value, segment_ids, grad_heads, HEADS_S, DH_S, student_scale)
    return (grad_query, grad_key, grad_value)
```

```python
import jax
import jax.numpy as jnp
from jax import lax
from jax.sharding import PartitionSpec as P

DH_T = 128
DH_S = 256
WINDOW = 1024


teacher_scale = 144.0 ** (-0.5)
negative = -1e30


def shifted(value, axis, by):
    length = lax.axis_size(axis)
    pairs = [(i, i + by) for i in range(length) if 0 <= i + by < length]
    return lax.ppermute(value, axis, pairs)


def swapped(value, axis, bit):
    length = lax.axis_size(axis)
    return lax.ppermute(value, axis, [(i, i ^ bit) for i in range(length)])


def gather_doubling(value, axis, along):
    size = lax.axis_size(axis)
    me = lax.axis_index(axis)
    bit = 1
    while bit < size:
        incoming = swapped(value, axis, bit)
        upper = (me // bit) % 2 == 1
        value = jnp.where(
            upper,
            jnp.concatenate([incoming, value], along),
            jnp.concatenate([value, incoming], along),
        )
        bit *= 2
    return value


def scatter_halving(value, axis):
    size = lax.axis_size(axis)
    me = lax.axis_index(axis)
    bit = size // 2
    while bit >= 1:
        half = value.shape[0] // 2
        low, high = value[:half], value[half:]
        upper = (me // bit) % 2 == 1
        send = jnp.where(upper, low, high)
        keep = jnp.where(upper, high, low)
        incoming = swapped(send.astype(jnp.bfloat16), axis, bit)
        value = keep + incoming.astype(jnp.float32)
        bit //= 2
    return value


def window_probs(queries, keys_all, marks_query, marks_all, heads, depth, scale, block_rows):
    query_part = queries.reshape(block_rows, heads, depth)
    key_part = keys_all.reshape(block_rows + WINDOW, heads, depth)
    scores = (
        jnp.einsum("qhd,khd->hqk", query_part, key_part, preferred_element_type=jnp.float32) * scale
    )
    row_index = lax.broadcasted_iota(jnp.int32, (block_rows, block_rows + WINDOW), 0)
    col_index = lax.broadcasted_iota(jnp.int32, (block_rows, block_rows + WINDOW), 1)
    same_doc = marks_query[:, None] == marks_all[None, :]
    allowed = same_doc & (col_index > row_index) & (col_index <= row_index + WINDOW)
    highest = jnp.max(jnp.where(allowed[None], scores, negative), axis=-1, keepdims=True)
    weights = jnp.where(allowed[None], jnp.exp(scores - highest), 0.0)
    totals = jnp.sum(weights, axis=-1, keepdims=True)
    probability = weights / totals
    return (probability, query_part, key_part)


def mix_values(probability, values_all, block_rows, heads, depth):
    value_part = values_all.reshape(block_rows + WINDOW, heads, depth)
    rounded = probability.astype(jnp.bfloat16)
    mixed = jnp.einsum("hqk,khd->qhd", rounded, value_part, preferred_element_type=jnp.float32)
    return (mixed.astype(jnp.bfloat16).reshape(block_rows, heads * depth), rounded, value_part)


def shards(
    teacher_query,
    teacher_key,
    teacher_value,
    student_query,
    student_key,
    student_value,
    segment_ids,
    language_ids,
    language_weight,
    teacher_out_proj,
    student_out_proj,
    match_proj,
):
    rows = teacher_query.shape[0]
    width = teacher_key.shape[1]
    reach = WINDOW // rows
    steps = reach // 2
    heads_t = teacher_query.shape[1] // DH_T
    heads_s = student_query.shape[1] // DH_S
    student_scale = DH_S ** (-0.5)
    doc_marks = segment_ids + 1
    mark_rows = jnp.pad(doc_marks.astype(jnp.bfloat16), (0, 8 * width - rows)).reshape(8, width)
    own = jnp.concatenate([teacher_key, teacher_value, student_key, student_value, mark_rows], 0)
    chain = [own]
    for _ in range(steps):
        chain.append(shifted(chain[-1], "seq", 2))
    core = lax.axis_index("seq") % 2
    stacked = jnp.stack(chain)
    partner = swapped(lax.dynamic_slice_in_dim(stacked, core, steps, 0), "seq", 1)
    pieces = []
    for k in range(steps, 0, -1):
        pieces.append(chain[k])
        pieces.append(partner[k - 1])
    pieces.append(own)
    window = jnp.stack(pieces)
    span = window.shape[0] * rows
    keys_teacher = window[:, 0:rows].reshape(span, width)
    values_teacher = window[:, rows : 2 * rows].reshape(span, width)
    keys_student = window[:, 2 * rows : 3 * rows].reshape(span, width)
    values_student = window[:, 3 * rows : 4 * rows].reshape(span, width)
    marks_all = (
        window[:, 4 * rows :].reshape(window.shape[0], 8 * width)[:, :rows].reshape(span)
    ).astype(jnp.int32)

    probability, _, _ = window_probs(
        teacher_query, keys_teacher, doc_marks, marks_all, heads_t, DH_T, teacher_scale, rows
    )
    teacher_mix, _, _ = mix_values(probability, values_teacher, rows, heads_t, DH_T)
    target_cols = lax.dot_general(
        gather_doubling(teacher_mix, "head", 1),
        teacher_out_proj,
        (((1,), (1,)), ((), ())),
        preferred_element_type=jnp.float32,
    ).astype(jnp.bfloat16)

    probability, query_part, key_part = window_probs(
        student_query, keys_student, doc_marks, marks_all, heads_s, DH_S, student_scale, rows
    )
    student_mix, rounded, value_part = mix_values(
        probability, values_student, rows, heads_s, DH_S
    )
    share_rows = rows // lax.axis_size("head")
    residual = scatter_halving(
        jnp.dot(student_mix, student_out_proj, preferred_element_type=jnp.float32)
        - jnp.dot(target_cols, match_proj, preferred_element_type=jnp.float32),
        "head",
    )
    my_langs = lax.dynamic_slice_in_dim(
        language_ids, lax.axis_index("head") * share_rows, share_rows, 0
    )
    lang_table = lax.broadcasted_iota(jnp.int32, (share_rows, language_weight.shape[0]), 1)
    token_weight = jnp.sum(
        jnp.where(my_langs[:, None] == lang_table, language_weight[None, :], 0.0), axis=1
    )
    grad_mix = (token_weight[:, None] * residual).astype(jnp.bfloat16)
    grad_heads = lax.dot_general(
        gather_doubling(grad_mix, "head", 0),
        student_out_proj,
        (((1,), (1,)), ((), ())),
        preferred_element_type=jnp.float32,
    ).astype(jnp.bfloat16)

    grad_part = grad_heads.reshape(rows, heads_s, DH_S)
    grad_probs = jnp.einsum(
        "qhd,khd->hqk", grad_part, value_part, preferred_element_type=jnp.float32
    )
    inner = jnp.sum(probability * grad_probs, axis=-1, keepdims=True)
    grad_scores = (probability * (grad_probs - inner)).astype(jnp.bfloat16)
    grad_q = student_scale * jnp.einsum(
        "hqk,khd->qhd", grad_scores, key_part, preferred_element_type=jnp.float32
    )
    grad_k = student_scale * jnp.einsum(
        "hqk,qhd->khd", grad_scores, query_part, preferred_element_type=jnp.float32
    )
    grad_v = jnp.einsum("hqk,qhd->khd", rounded, grad_part, preferred_element_type=jnp.float32)
    blocks = span // rows
    grads = jnp.concatenate(
        [grad_k.reshape(blocks, rows, width), grad_v.reshape(blocks, rows, width)], 1
    )
    from_partner = swapped(grads[1::2], "seq", 1)
    nothing = jnp.zeros_like(from_partner[:1])
    added = jnp.where(
        core == 1,
        jnp.concatenate([from_partner, nothing], 0),
        jnp.concatenate([nothing, from_partner], 0),
    )
    even = grads[0::2] + added
    total = even[0]
    for k in range(1, steps + 1):
        total = even[k] + shifted(total.astype(jnp.bfloat16), "seq", -2).astype(jnp.float32)
    return (grad_q.reshape(rows, width), total[:rows], total[rows:])


def solution(mesh):
    in_specs = (
        P("seq", "head"),
        P("seq", "head"),
        P("seq", "head"),
        P("seq", "head"),
        P("seq", "head"),
        P("seq", "head"),
        P("seq"),
        P("seq"),
        P(),
        P("head", None),
        P("head", None),
        P("head", None),
    )
    out_specs = (P("seq", "head"), P("seq", "head"), P("seq", "head"))
    return jax.shard_map(shards, mesh=mesh, in_specs=in_specs, out_specs=out_specs, check_vma=False)
```

```python
import jax
import jax.numpy as jnp
from jax import lax
from jax.sharding import PartitionSpec as P

DH_T = 128
DH_S = 256
WINDOW = 1024


teacher_scale = 144.0 ** (-0.5)
negative = -1e30


def shifted(value, axis, by):
    length = lax.axis_size(axis)
    pairs = [(i, i + by) for i in range(length) if 0 <= i + by < length]
    return lax.ppermute(value, axis, pairs)


def swapped(value, axis, bit):
    length = lax.axis_size(axis)
    return lax.ppermute(value, axis, [(i, i ^ bit) for i in range(length)])


def rotated(value, axis, by):
    length = lax.axis_size(axis)
    return lax.ppermute(value, axis, [(i, (i + by) % length) for i in range(length)])


def gather_direct(value, axis, along):
    size = lax.axis_size(axis)
    me = lax.axis_index(axis)
    got = [value] + [rotated(value, axis, by) for by in range(1, size)]
    ordered = jnp.stack([got[(-by) % size] for by in range(size)])
    placed = jnp.roll(ordered, me, axis=0)
    return jnp.concatenate([placed[j] for j in range(size)], along)


def scatter_direct(value, axis):
    size = lax.axis_size(axis)
    me = lax.axis_index(axis)
    blocks = value.reshape(size, value.shape[0] // size, value.shape[1])
    total = lax.dynamic_index_in_dim(blocks, me, 0, keepdims=False)
    for by in range(1, size):
        send = lax.dynamic_index_in_dim(blocks, (me + by) % size, 0, keepdims=False)
        total = total + rotated(send.astype(jnp.bfloat16), axis, by).astype(jnp.float32)
    return total


def window_probs(queries, keys_all, marks_query, marks_all, heads, depth, scale, block_rows):
    query_part = queries.reshape(block_rows, heads, depth)
    key_part = keys_all.reshape(block_rows + WINDOW, heads, depth)
    scores = (
        jnp.einsum("qhd,khd->hqk", query_part, key_part, preferred_element_type=jnp.float32) * scale
    )
    row_index = lax.broadcasted_iota(jnp.int32, (block_rows, block_rows + WINDOW), 0)
    col_index = lax.broadcasted_iota(jnp.int32, (block_rows, block_rows + WINDOW), 1)
    same_doc = marks_query[:, None] == marks_all[None, :]
    allowed = same_doc & (col_index > row_index) & (col_index <= row_index + WINDOW)
    highest = jnp.max(jnp.where(allowed[None], scores, negative), axis=-1, keepdims=True)
    weights = jnp.where(allowed[None], jnp.exp(scores - highest), 0.0)
    totals = jnp.sum(weights, axis=-1, keepdims=True)
    probability = weights / totals
    return (probability, query_part, key_part)


def mix_values(probability, values_all, block_rows, heads, depth):
    value_part = values_all.reshape(block_rows + WINDOW, heads, depth)
    rounded = probability.astype(jnp.bfloat16)
    mixed = jnp.einsum("hqk,khd->qhd", rounded, value_part, preferred_element_type=jnp.float32)
    return (mixed.astype(jnp.bfloat16).reshape(block_rows, heads * depth), rounded, value_part)


def shards(
    teacher_query,
    teacher_key,
    teacher_value,
    student_query,
    student_key,
    student_value,
    segment_ids,
    language_ids,
    language_weight,
    teacher_out_proj,
    student_out_proj,
    match_proj,
):
    rows = teacher_query.shape[0]
    width = teacher_key.shape[1]
    reach = WINDOW // rows
    steps = reach // 2
    heads_t = teacher_query.shape[1] // DH_T
    heads_s = student_query.shape[1] // DH_S
    student_scale = DH_S ** (-0.5)
    doc_marks = segment_ids + 1
    mark_rows = jnp.pad(doc_marks.astype(jnp.bfloat16), (0, 8 * width - rows)).reshape(8, width)
    own = jnp.concatenate([teacher_key, teacher_value, student_key, student_value, mark_rows], 0)
    chain = [own]
    for _ in range(steps):
        chain.append(shifted(chain[-1], "seq", 2))
    core = lax.axis_index("seq") % 2
    stacked = jnp.stack(chain)
    partner = swapped(lax.dynamic_slice_in_dim(stacked, core, steps, 0), "seq", 1)
    pieces = []
    for k in range(steps, 0, -1):
        pieces.append(chain[k])
        pieces.append(partner[k - 1])
    pieces.append(own)
    window = jnp.stack(pieces)
    span = window.shape[0] * rows
    keys_teacher = window[:, 0:rows].reshape(span, width)
    values_teacher = window[:, rows : 2 * rows].reshape(span, width)
    keys_student = window[:, 2 * rows : 3 * rows].reshape(span, width)
    values_student = window[:, 3 * rows : 4 * rows].reshape(span, width)
    marks_all = (
        window[:, 4 * rows :].reshape(window.shape[0], 8 * width)[:, :rows].reshape(span)
    ).astype(jnp.int32)

    probability, _, _ = window_probs(
        teacher_query, keys_teacher, doc_marks, marks_all, heads_t, DH_T, teacher_scale, rows
    )
    teacher_mix, _, _ = mix_values(probability, values_teacher, rows, heads_t, DH_T)
    target_cols = lax.dot_general(
        gather_direct(teacher_mix, "head", 1),
        teacher_out_proj,
        (((1,), (1,)), ((), ())),
        preferred_element_type=jnp.float32,
    ).astype(jnp.bfloat16)

    probability, query_part, key_part = window_probs(
        student_query, keys_student, doc_marks, marks_all, heads_s, DH_S, student_scale, rows
    )
    student_mix, rounded, value_part = mix_values(
        probability, values_student, rows, heads_s, DH_S
    )
    share_rows = rows // lax.axis_size("head")
    residual = scatter_direct(
        jnp.dot(student_mix, student_out_proj, preferred_element_type=jnp.float32)
        - jnp.dot(target_cols, match_proj, preferred_element_type=jnp.float32),
        "head",
    )
    my_langs = lax.dynamic_slice_in_dim(
        language_ids, lax.axis_index("head") * share_rows, share_rows, 0
    )
    lang_table = lax.broadcasted_iota(jnp.int32, (share_rows, language_weight.shape[0]), 1)
    token_weight = jnp.sum(
        jnp.where(my_langs[:, None] == lang_table, language_weight[None, :], 0.0), axis=1
    )
    grad_mix = (token_weight[:, None] * residual).astype(jnp.bfloat16)
    grad_heads = lax.dot_general(
        gather_direct(grad_mix, "head", 0),
        student_out_proj,
        (((1,), (1,)), ((), ())),
        preferred_element_type=jnp.float32,
    ).astype(jnp.bfloat16)

    grad_part = grad_heads.reshape(rows, heads_s, DH_S)
    grad_probs = jnp.einsum(
        "qhd,khd->hqk", grad_part, value_part, preferred_element_type=jnp.float32
    )
    inner = jnp.sum(probability * grad_probs, axis=-1, keepdims=True)
    grad_scores = (probability * (grad_probs - inner)).astype(jnp.bfloat16)
    grad_q = student_scale * jnp.einsum(
        "hqk,khd->qhd", grad_scores, key_part, preferred_element_type=jnp.float32
    )
    grad_k = student_scale * jnp.einsum(
        "hqk,qhd->khd", grad_scores, query_part, preferred_element_type=jnp.float32
    )
    grad_v = jnp.einsum("hqk,qhd->khd", rounded, grad_part, preferred_element_type=jnp.float32)
    blocks = span // rows
    grads = jnp.concatenate(
        [grad_k.reshape(blocks, rows, width), grad_v.reshape(blocks, rows, width)], 1
    )
    from_partner = swapped(grads[1::2], "seq", 1)
    nothing = jnp.zeros_like(from_partner[:1])
    added = jnp.where(
        core == 1,
        jnp.concatenate([from_partner, nothing], 0),
        jnp.concatenate([nothing, from_partner], 0),
    )
    even = grads[0::2] + added
    total = even[0]
    for k in range(1, steps + 1):
        total = even[k] + shifted(total.astype(jnp.bfloat16), "seq", -2).astype(jnp.float32)
    return (grad_q.reshape(rows, width), total[:rows], total[rows:])


def solution(mesh):
    in_specs = (
        P("seq", "head"),
        P("seq", "head"),
        P("seq", "head"),
        P("seq", "head"),
        P("seq", "head"),
        P("seq", "head"),
        P("seq"),
        P("seq"),
        P(),
        P("head", None),
        P("head", None),
        P("head", None),
    )
    out_specs = (P("seq", "head"), P("seq", "head"), P("seq", "head"))
    return jax.shard_map(shards, mesh=mesh, in_specs=in_specs, out_specs=out_specs, check_vma=False)
```

```python
import jax
import jax.numpy as jnp
from jax import lax
from jax.sharding import PartitionSpec as P

DH_T = 128
DH_S = 256
WINDOW = 1024


teacher_scale = 144.0 ** (-0.5)
negative = -1e30


def shifted(value, axis, by):
    length = lax.axis_size(axis)
    pairs = [(i, i + by) for i in range(length) if 0 <= i + by < length]
    return lax.ppermute(value, axis, pairs)


def swapped(value, axis, bit):
    length = lax.axis_size(axis)
    return lax.ppermute(value, axis, [(i, i ^ bit) for i in range(length)])


def gather_doubling(value, axis, along):
    size = lax.axis_size(axis)
    me = lax.axis_index(axis)
    bit = 1
    while bit < size:
        incoming = swapped(value, axis, bit)
        upper = (me // bit) % 2 == 1
        value = jnp.where(
            upper,
            jnp.concatenate([incoming, value], along),
            jnp.concatenate([value, incoming], along),
        )
        bit *= 2
    return value


def scatter_halving(value, axis):
    size = lax.axis_size(axis)
    me = lax.axis_index(axis)
    bit = size // 2
    while bit >= 1:
        half = value.shape[0] // 2
        low, high = value[:half], value[half:]
        upper = (me // bit) % 2 == 1
        send = jnp.where(upper, low, high)
        keep = jnp.where(upper, high, low)
        incoming = swapped(send.astype(jnp.bfloat16), axis, bit)
        value = keep + incoming.astype(jnp.float32)
        bit //= 2
    return value


def reduce_doubling(value, axis):
    size = lax.axis_size(axis)
    bit = 1
    while bit < size:
        value = value + swapped(value.astype(jnp.bfloat16), axis, bit).astype(jnp.float32)
        bit *= 2
    return value


def window_probs(queries, keys_all, marks_query, marks_all, heads, depth, scale, block_rows):
    query_part = queries.reshape(block_rows, heads, depth)
    key_part = keys_all.reshape(block_rows + WINDOW, heads, depth)
    scores = (
        jnp.einsum("qhd,khd->hqk", query_part, key_part, preferred_element_type=jnp.float32) * scale
    )
    row_index = lax.broadcasted_iota(jnp.int32, (block_rows, block_rows + WINDOW), 0)
    col_index = lax.broadcasted_iota(jnp.int32, (block_rows, block_rows + WINDOW), 1)
    same_doc = marks_query[:, None] == marks_all[None, :]
    allowed = same_doc & (col_index > row_index) & (col_index <= row_index + WINDOW)
    highest = jnp.max(jnp.where(allowed[None], scores, negative), axis=-1, keepdims=True)
    weights = jnp.where(allowed[None], jnp.exp(scores - highest), 0.0)
    totals = jnp.sum(weights, axis=-1, keepdims=True)
    probability = weights / totals
    return (probability, query_part, key_part)


def mix_values(probability, values_all, block_rows, heads, depth):
    value_part = values_all.reshape(block_rows + WINDOW, heads, depth)
    rounded = probability.astype(jnp.bfloat16)
    mixed = jnp.einsum("hqk,khd->qhd", rounded, value_part, preferred_element_type=jnp.float32)
    return (mixed.astype(jnp.bfloat16).reshape(block_rows, heads * depth), rounded, value_part)


def shards(
    teacher_query,
    teacher_key,
    teacher_value,
    student_query,
    student_key,
    student_value,
    segment_ids,
    language_ids,
    language_weight,
    teacher_out_proj,
    student_out_proj,
    match_proj,
):
    rows = teacher_query.shape[0]
    width = teacher_key.shape[1]
    reach = WINDOW // rows
    steps = reach // 2
    heads_t = teacher_query.shape[1] // DH_T
    heads_s = student_query.shape[1] // DH_S
    student_scale = DH_S ** (-0.5)
    doc_marks = segment_ids + 1
    mark_rows = jnp.pad(doc_marks.astype(jnp.bfloat16), (0, 8 * width - rows)).reshape(8, width)
    own = jnp.concatenate([teacher_key, teacher_value, student_key, student_value, mark_rows], 0)
    chain = [own]
    for _ in range(steps):
        chain.append(shifted(chain[-1], "seq", 2))
    core = lax.axis_index("seq") % 2
    stacked = jnp.stack(chain)
    partner = swapped(lax.dynamic_slice_in_dim(stacked, core, steps, 0), "seq", 1)
    pieces = []
    for k in range(steps, 0, -1):
        pieces.append(chain[k])
        pieces.append(partner[k - 1])
    pieces.append(own)
    window = jnp.stack(pieces)
    span = window.shape[0] * rows
    keys_teacher = window[:, 0:rows].reshape(span, width)
    values_teacher = window[:, rows : 2 * rows].reshape(span, width)
    keys_student = window[:, 2 * rows : 3 * rows].reshape(span, width)
    values_student = window[:, 3 * rows : 4 * rows].reshape(span, width)
    marks_all = (
        window[:, 4 * rows :].reshape(window.shape[0], 8 * width)[:, :rows].reshape(span)
    ).astype(jnp.int32)

    probability, _, _ = window_probs(
        teacher_query, keys_teacher, doc_marks, marks_all, heads_t, DH_T, teacher_scale, rows
    )
    teacher_mix, _, _ = mix_values(probability, values_teacher, rows, heads_t, DH_T)
    target_cols = lax.dot_general(
        gather_doubling(teacher_mix, "head", 1),
        teacher_out_proj,
        (((1,), (1,)), ((), ())),
        preferred_element_type=jnp.float32,
    ).astype(jnp.bfloat16)

    probability, query_part, key_part = window_probs(
        student_query, keys_student, doc_marks, marks_all, heads_s, DH_S, student_scale, rows
    )
    student_mix, rounded, value_part = mix_values(
        probability, values_student, rows, heads_s, DH_S
    )
    lang_table = lax.broadcasted_iota(jnp.int32, (rows, language_weight.shape[0]), 1)
    token_weight = jnp.sum(
        jnp.where(language_ids[:, None] == lang_table, language_weight[None, :], 0.0), axis=1
    )
    weighted = token_weight[:, None] * (
        jnp.dot(student_mix, student_out_proj, preferred_element_type=jnp.float32)
        - jnp.dot(target_cols, match_proj, preferred_element_type=jnp.float32)
    )
    grad_mix = reduce_doubling(weighted, "head").astype(jnp.bfloat16)
    grad_heads = lax.dot_general(
        grad_mix,
        student_out_proj,
        (((1,), (1,)), ((), ())),
        preferred_element_type=jnp.float32,
    ).astype(jnp.bfloat16)

    grad_part = grad_heads.reshape(rows, heads_s, DH_S)
    grad_probs = jnp.einsum(
        "qhd,khd->hqk", grad_part, value_part, preferred_element_type=jnp.float32
    )
    inner = jnp.sum(probability * grad_probs, axis=-1, keepdims=True)
    grad_scores = (probability * (grad_probs - inner)).astype(jnp.bfloat16)
    grad_q = student_scale * jnp.einsum(
        "hqk,khd->qhd", grad_scores, key_part, preferred_element_type=jnp.float32
    )
    grad_k = student_scale * jnp.einsum(
        "hqk,qhd->khd", grad_scores, query_part, preferred_element_type=jnp.float32
    )
    grad_v = jnp.einsum("hqk,qhd->khd", rounded, grad_part, preferred_element_type=jnp.float32)
    blocks = span // rows
    grads = jnp.concatenate(
        [grad_k.reshape(blocks, rows, width), grad_v.reshape(blocks, rows, width)], 1
    )
    from_partner = swapped(grads[1::2], "seq", 1)
    nothing = jnp.zeros_like(from_partner[:1])
    added = jnp.where(
        core == 1,
        jnp.concatenate([from_partner, nothing], 0),
        jnp.concatenate([nothing, from_partner], 0),
    )
    even = grads[0::2] + added
    total = even[0]
    for k in range(1, steps + 1):
        total = even[k] + shifted(total.astype(jnp.bfloat16), "seq", -2).astype(jnp.float32)
    return (grad_q.reshape(rows, width), total[:rows], total[rows:])


def solution(mesh):
    in_specs = (
        P("seq", "head"),
        P("seq", "head"),
        P("seq", "head"),
        P("seq", "head"),
        P("seq", "head"),
        P("seq", "head"),
        P("seq"),
        P("seq"),
        P(),
        P("head", None),
        P("head", None),
        P("head", None),
    )
    out_specs = (P("seq", "head"), P("seq", "head"), P("seq", "head"))
    return jax.shard_map(shards, mesh=mesh, in_specs=in_specs, out_specs=out_specs, check_vma=False)
```

```python
import jax
import jax.numpy as jnp
from jax import lax
from jax.sharding import PartitionSpec as P

DH_T = 128
DH_S = 256
WINDOW = 1024


teacher_scale = 144.0 ** (-0.5)
negative = -1e30


def shifted(value, axis, by):
    length = lax.axis_size(axis)
    pairs = [(i, i + by) for i in range(length) if 0 <= i + by < length]
    return lax.ppermute(value, axis, pairs)


def swapped(value, axis, bit):
    length = lax.axis_size(axis)
    return lax.ppermute(value, axis, [(i, i ^ bit) for i in range(length)])


def gather_doubling(value, axis, along):
    size = lax.axis_size(axis)
    me = lax.axis_index(axis)
    bit = 1
    while bit < size:
        incoming = swapped(value, axis, bit)
        upper = (me // bit) % 2 == 1
        value = jnp.where(
            upper,
            jnp.concatenate([incoming, value], along),
            jnp.concatenate([value, incoming], along),
        )
        bit *= 2
    return value


def scatter_halving(value, axis):
    size = lax.axis_size(axis)
    me = lax.axis_index(axis)
    bit = size // 2
    while bit >= 1:
        half = value.shape[0] // 2
        low, high = value[:half], value[half:]
        upper = (me // bit) % 2 == 1
        send = jnp.where(upper, low, high)
        keep = jnp.where(upper, high, low)
        incoming = swapped(send.astype(jnp.bfloat16), axis, bit)
        value = keep + incoming.astype(jnp.float32)
        bit //= 2
    return value


def reduce_doubling(value, axis):
    size = lax.axis_size(axis)
    bit = 1
    while bit < size:
        value = value + swapped(value.astype(jnp.bfloat16), axis, bit).astype(jnp.float32)
        bit *= 2
    return value


def swap_pieces(chain, steps, core):
    partner = swapped(lax.dynamic_slice_in_dim(jnp.stack(chain), core, steps, 0), "seq", 1)
    pieces = []
    for k in range(steps, 0, -1):
        pieces.append(chain[k])
        pieces.append(partner[k - 1])
    pieces.append(chain[0])
    return pieces


def relay(own, steps, core):
    chain = [own]
    for _ in range(steps):
        chain.append(shifted(chain[-1], "seq", 2))
    return swap_pieces(chain, steps, core)


def gather_beside_relay(value, axis, along, own, steps):
    size = lax.axis_size(axis)
    me = lax.axis_index(axis)
    own, value = lax.optimization_barrier((own, value))
    chain = [own]
    bit = 1
    for _ in range(steps):
        if bit < size:
            incoming = swapped(value, axis, bit)
        step = shifted(chain[-1], "seq", 2)
        if bit < size:
            upper = (me // bit) % 2 == 1
            value = jnp.where(
                upper,
                jnp.concatenate([incoming, value], along),
                jnp.concatenate([value, incoming], along),
            )
            bit *= 2
        value, step = lax.optimization_barrier((value, step))
        chain.append(step)
    while bit < size:
        incoming = swapped(value, axis, bit)
        upper = (me // bit) % 2 == 1
        value = jnp.where(
            upper,
            jnp.concatenate([incoming, value], along),
            jnp.concatenate([value, incoming], along),
        )
        bit *= 2
    return value, chain


def joined(pieces, first, last):
    return jnp.concatenate([piece[first:last] for piece in pieces], 0)


def window_probs(queries, keys_all, marks_query, marks_all, heads, depth, scale, block_rows):
    query_part = queries.reshape(block_rows, heads, depth)
    key_part = keys_all.reshape(block_rows + WINDOW, heads, depth)
    scores = (
        jnp.einsum("qhd,khd->hqk", query_part, key_part, preferred_element_type=jnp.float32) * scale
    )
    row_index = lax.broadcasted_iota(jnp.int32, (block_rows, block_rows + WINDOW), 0)
    col_index = lax.broadcasted_iota(jnp.int32, (block_rows, block_rows + WINDOW), 1)
    same_doc = marks_query[:, None] == marks_all[None, :]
    allowed = same_doc & (col_index > row_index) & (col_index <= row_index + WINDOW)
    highest = jnp.max(jnp.where(allowed[None], scores, negative), axis=-1, keepdims=True)
    weights = jnp.where(allowed[None], jnp.exp(scores - highest), 0.0)
    totals = jnp.sum(weights, axis=-1, keepdims=True)
    probability = weights / totals
    return (probability, query_part, key_part)


def mix_values(probability, values_all, block_rows, heads, depth):
    value_part = values_all.reshape(block_rows + WINDOW, heads, depth)
    rounded = probability.astype(jnp.bfloat16)
    mixed = jnp.einsum("hqk,khd->qhd", rounded, value_part, preferred_element_type=jnp.float32)
    return (mixed.astype(jnp.bfloat16).reshape(block_rows, heads * depth), rounded, value_part)


def shards(
    teacher_query,
    teacher_key,
    teacher_value,
    student_query,
    student_key,
    student_value,
    segment_ids,
    language_ids,
    language_weight,
    teacher_out_proj,
    student_out_proj,
    match_proj,
):
    rows = teacher_query.shape[0]
    width = teacher_key.shape[1]
    reach = WINDOW // rows
    steps = reach // 2
    heads_t = teacher_query.shape[1] // DH_T
    heads_s = student_query.shape[1] // DH_S
    student_scale = DH_S ** (-0.5)
    doc_marks = segment_ids + 1
    mark_rows = jnp.pad(doc_marks.astype(jnp.bfloat16), (0, 8 * width - rows)).reshape(8, width)
    core = lax.axis_index("seq") % 2
    own_teacher = jnp.concatenate([teacher_key, teacher_value, mark_rows], 0)
    pieces_teacher = relay(own_teacher, steps, core)
    keys_teacher = joined(pieces_teacher, 0, rows)
    values_teacher = joined(pieces_teacher, rows, 2 * rows)
    marks_all = jnp.concatenate(
        [piece[2 * rows :].reshape(8 * width)[:rows] for piece in pieces_teacher], 0
    ).astype(jnp.int32)

    probability, _, _ = window_probs(
        teacher_query, keys_teacher, doc_marks, marks_all, heads_t, DH_T, teacher_scale, rows
    )
    teacher_mix, _, _ = mix_values(probability, values_teacher, rows, heads_t, DH_T)
    own_student = jnp.concatenate([student_key, student_value], 0)
    gathered, chain_student = gather_beside_relay(teacher_mix, "head", 1, own_student, steps)
    pieces_student = swap_pieces(chain_student, steps, core)
    keys_student = joined(pieces_student, 0, rows)
    values_student = joined(pieces_student, rows, 2 * rows)
    target_cols = lax.dot_general(
        gathered,
        teacher_out_proj,
        (((1,), (1,)), ((), ())),
        preferred_element_type=jnp.float32,
    ).astype(jnp.bfloat16)

    probability, query_part, key_part = window_probs(
        student_query, keys_student, doc_marks, marks_all, heads_s, DH_S, student_scale, rows
    )
    student_mix, rounded, value_part = mix_values(
        probability, values_student, rows, heads_s, DH_S
    )
    lang_table = lax.broadcasted_iota(jnp.int32, (rows, language_weight.shape[0]), 1)
    token_weight = jnp.sum(
        jnp.where(language_ids[:, None] == lang_table, language_weight[None, :], 0.0), axis=1
    )
    weighted = token_weight[:, None] * (
        jnp.dot(student_mix, student_out_proj, preferred_element_type=jnp.float32)
        - jnp.dot(target_cols, match_proj, preferred_element_type=jnp.float32)
    )
    grad_mix = reduce_doubling(weighted, "head").astype(jnp.bfloat16)
    grad_heads = lax.dot_general(
        grad_mix,
        student_out_proj,
        (((1,), (1,)), ((), ())),
        preferred_element_type=jnp.float32,
    ).astype(jnp.bfloat16)

    grad_part = grad_heads.reshape(rows, heads_s, DH_S)
    grad_probs = jnp.einsum(
        "qhd,khd->hqk", grad_part, value_part, preferred_element_type=jnp.float32
    )
    inner = jnp.sum(probability * grad_probs, axis=-1, keepdims=True)
    grad_scores = (probability * (grad_probs - inner)).astype(jnp.bfloat16)
    grad_q = student_scale * jnp.einsum(
        "hqk,khd->qhd", grad_scores, key_part, preferred_element_type=jnp.float32
    )
    grad_k = student_scale * jnp.einsum(
        "hqk,qhd->khd", grad_scores, query_part, preferred_element_type=jnp.float32
    )
    grad_v = jnp.einsum("hqk,qhd->khd", rounded, grad_part, preferred_element_type=jnp.float32)
    blocks = keys_student.shape[0] // rows
    grads = jnp.concatenate(
        [grad_k.reshape(blocks, rows, width), grad_v.reshape(blocks, rows, width)], 1
    )
    from_partner = swapped(grads[1::2], "seq", 1)
    nothing = jnp.zeros_like(from_partner[:1])
    added = jnp.where(
        core == 1,
        jnp.concatenate([from_partner, nothing], 0),
        jnp.concatenate([nothing, from_partner], 0),
    )
    even = grads[0::2] + added
    total = even[0]
    for k in range(1, steps + 1):
        total = even[k] + shifted(total.astype(jnp.bfloat16), "seq", -2).astype(jnp.float32)
    return (grad_q.reshape(rows, width), total[:rows], total[rows:])


def solution(mesh):
    in_specs = (
        P("seq", "head"),
        P("seq", "head"),
        P("seq", "head"),
        P("seq", "head"),
        P("seq", "head"),
        P("seq", "head"),
        P("seq"),
        P("seq"),
        P(),
        P("head", None),
        P("head", None),
        P("head", None),
    )
    out_specs = (P("seq", "head"), P("seq", "head"), P("seq", "head"))
    return jax.shard_map(shards, mesh=mesh, in_specs=in_specs, out_specs=out_specs, check_vma=False)
```

```python
import jax
import jax.numpy as jnp
from jax import lax
from jax.sharding import PartitionSpec as P

DH_T = 128
DH_S = 256
WINDOW = 1024


teacher_scale = 144.0 ** (-0.5)
negative = -1e30


def shifted(value, axis, by):
    length = lax.axis_size(axis)
    pairs = [(i, i + by) for i in range(length) if 0 <= i + by < length]
    return lax.ppermute(value, axis, pairs)


def swapped(value, axis, bit):
    length = lax.axis_size(axis)
    return lax.ppermute(value, axis, [(i, i ^ bit) for i in range(length)])


def gather_doubling(value, axis, along):
    size = lax.axis_size(axis)
    me = lax.axis_index(axis)
    bit = 1
    while bit < size:
        incoming = swapped(value, axis, bit)
        upper = (me // bit) % 2 == 1
        value = jnp.where(
            upper,
            jnp.concatenate([incoming, value], along),
            jnp.concatenate([value, incoming], along),
        )
        bit *= 2
    return value


def scatter_halving(value, axis):
    size = lax.axis_size(axis)
    me = lax.axis_index(axis)
    bit = size // 2
    while bit >= 1:
        half = value.shape[0] // 2
        low, high = value[:half], value[half:]
        upper = (me // bit) % 2 == 1
        send = jnp.where(upper, low, high)
        keep = jnp.where(upper, high, low)
        incoming = swapped(send.astype(jnp.bfloat16), axis, bit)
        value = keep + incoming.astype(jnp.float32)
        bit //= 2
    return value


def reduce_in_halves(value, axis):
    size = lax.axis_size(axis)
    me = lax.axis_index(axis)
    top = size // 2
    half = value.shape[0] // 2
    upper = (me // top) % 2 == 1
    send = jnp.where(upper, value[:half], value[half:])
    keep = jnp.where(upper, value[half:], value[:half])
    part = keep + swapped(send.astype(jnp.bfloat16), axis, top).astype(jnp.float32)
    bit = 1
    while bit < top:
        part = part + swapped(part.astype(jnp.bfloat16), axis, bit).astype(jnp.float32)
        bit *= 2
    part = part.astype(jnp.bfloat16)
    other = swapped(part, axis, top)
    return jnp.where(
        upper, jnp.concatenate([other, part], 0), jnp.concatenate([part, other], 0)
    )


def window_probs(queries, keys_all, marks_query, marks_all, heads, depth, scale, block_rows):
    query_part = queries.reshape(block_rows, heads, depth)
    key_part = keys_all.reshape(block_rows + WINDOW, heads, depth)
    scores = (
        jnp.einsum("qhd,khd->hqk", query_part, key_part, preferred_element_type=jnp.float32) * scale
    )
    row_index = lax.broadcasted_iota(jnp.int32, (block_rows, block_rows + WINDOW), 0)
    col_index = lax.broadcasted_iota(jnp.int32, (block_rows, block_rows + WINDOW), 1)
    same_doc = marks_query[:, None] == marks_all[None, :]
    allowed = same_doc & (col_index > row_index) & (col_index <= row_index + WINDOW)
    highest = jnp.max(jnp.where(allowed[None], scores, negative), axis=-1, keepdims=True)
    weights = jnp.where(allowed[None], jnp.exp(scores - highest), 0.0)
    totals = jnp.sum(weights, axis=-1, keepdims=True)
    probability = weights / totals
    return (probability, query_part, key_part)


def mix_values(probability, values_all, block_rows, heads, depth):
    value_part = values_all.reshape(block_rows + WINDOW, heads, depth)
    rounded = probability.astype(jnp.bfloat16)
    mixed = jnp.einsum("hqk,khd->qhd", rounded, value_part, preferred_element_type=jnp.float32)
    return (mixed.astype(jnp.bfloat16).reshape(block_rows, heads * depth), rounded, value_part)


def shards(
    teacher_query,
    teacher_key,
    teacher_value,
    student_query,
    student_key,
    student_value,
    segment_ids,
    language_ids,
    language_weight,
    teacher_out_proj,
    student_out_proj,
    match_proj,
):
    rows = teacher_query.shape[0]
    width = teacher_key.shape[1]
    reach = WINDOW // rows
    steps = reach // 2
    heads_t = teacher_query.shape[1] // DH_T
    heads_s = student_query.shape[1] // DH_S
    student_scale = DH_S ** (-0.5)
    doc_marks = segment_ids + 1
    mark_rows = jnp.pad(doc_marks.astype(jnp.bfloat16), (0, 8 * width - rows)).reshape(8, width)
    own = jnp.concatenate([teacher_key, teacher_value, student_key, student_value, mark_rows], 0)
    chain = [own]
    for _ in range(steps):
        chain.append(shifted(chain[-1], "seq", 2))
    core = lax.axis_index("seq") % 2
    stacked = jnp.stack(chain)
    partner = swapped(lax.dynamic_slice_in_dim(stacked, core, steps, 0), "seq", 1)
    pieces = []
    for k in range(steps, 0, -1):
        pieces.append(chain[k])
        pieces.append(partner[k - 1])
    pieces.append(own)
    window = jnp.stack(pieces)
    span = window.shape[0] * rows
    keys_teacher = window[:, 0:rows].reshape(span, width)
    values_teacher = window[:, rows : 2 * rows].reshape(span, width)
    keys_student = window[:, 2 * rows : 3 * rows].reshape(span, width)
    values_student = window[:, 3 * rows : 4 * rows].reshape(span, width)
    marks_all = (
        window[:, 4 * rows :].reshape(window.shape[0], 8 * width)[:, :rows].reshape(span)
    ).astype(jnp.int32)

    probability, _, _ = window_probs(
        teacher_query, keys_teacher, doc_marks, marks_all, heads_t, DH_T, teacher_scale, rows
    )
    teacher_mix, _, _ = mix_values(probability, values_teacher, rows, heads_t, DH_T)
    target_cols = lax.dot_general(
        gather_doubling(teacher_mix, "head", 1),
        teacher_out_proj,
        (((1,), (1,)), ((), ())),
        preferred_element_type=jnp.float32,
    ).astype(jnp.bfloat16)

    probability, query_part, key_part = window_probs(
        student_query, keys_student, doc_marks, marks_all, heads_s, DH_S, student_scale, rows
    )
    student_mix, rounded, value_part = mix_values(
        probability, values_student, rows, heads_s, DH_S
    )
    lang_table = lax.broadcasted_iota(jnp.int32, (rows, language_weight.shape[0]), 1)
    token_weight = jnp.sum(
        jnp.where(language_ids[:, None] == lang_table, language_weight[None, :], 0.0), axis=1
    )
    weighted = token_weight[:, None] * (
        jnp.dot(student_mix, student_out_proj, preferred_element_type=jnp.float32)
        - jnp.dot(target_cols, match_proj, preferred_element_type=jnp.float32)
    )
    grad_mix = reduce_in_halves(weighted, "head")
    grad_heads = lax.dot_general(
        grad_mix,
        student_out_proj,
        (((1,), (1,)), ((), ())),
        preferred_element_type=jnp.float32,
    ).astype(jnp.bfloat16)

    grad_part = grad_heads.reshape(rows, heads_s, DH_S)
    grad_probs = jnp.einsum(
        "qhd,khd->hqk", grad_part, value_part, preferred_element_type=jnp.float32
    )
    inner = jnp.sum(probability * grad_probs, axis=-1, keepdims=True)
    grad_scores = (probability * (grad_probs - inner)).astype(jnp.bfloat16)
    grad_q = student_scale * jnp.einsum(
        "hqk,khd->qhd", grad_scores, key_part, preferred_element_type=jnp.float32
    )
    grad_k = student_scale * jnp.einsum(
        "hqk,qhd->khd", grad_scores, query_part, preferred_element_type=jnp.float32
    )
    grad_v = jnp.einsum("hqk,qhd->khd", rounded, grad_part, preferred_element_type=jnp.float32)
    blocks = span // rows
    grads = jnp.concatenate(
        [grad_k.reshape(blocks, rows, width), grad_v.reshape(blocks, rows, width)], 1
    )
    from_partner = swapped(grads[1::2], "seq", 1)
    nothing = jnp.zeros_like(from_partner[:1])
    added = jnp.where(
        core == 1,
        jnp.concatenate([from_partner, nothing], 0),
        jnp.concatenate([nothing, from_partner], 0),
    )
    even = grads[0::2] + added
    total = even[0]
    for k in range(1, steps + 1):
        total = even[k] + shifted(total.astype(jnp.bfloat16), "seq", -2).astype(jnp.float32)
    return (grad_q.reshape(rows, width), total[:rows], total[rows:])


def solution(mesh):
    in_specs = (
        P("seq", "head"),
        P("seq", "head"),
        P("seq", "head"),
        P("seq", "head"),
        P("seq", "head"),
        P("seq", "head"),
        P("seq"),
        P("seq"),
        P(),
        P("head", None),
        P("head", None),
        P("head", None),
    )
    out_specs = (P("seq", "head"), P("seq", "head"), P("seq", "head"))
    return jax.shard_map(shards, mesh=mesh, in_specs=in_specs, out_specs=out_specs, check_vma=False)
```

```python
import jax
import jax.numpy as jnp
from jax import lax
from jax.sharding import PartitionSpec as P

DH_T = 128
DH_S = 256
WINDOW = 1024


teacher_scale = 144.0 ** (-0.5)
negative = -1e30


def shifted(value, axis, by):
    length = lax.axis_size(axis)
    pairs = [(i, i + by) for i in range(length) if 0 <= i + by < length]
    return lax.ppermute(value, axis, pairs)


def swapped(value, axis, bit):
    length = lax.axis_size(axis)
    return lax.ppermute(value, axis, [(i, i ^ bit) for i in range(length)])


def gather_doubling(value, axis, along):
    size = lax.axis_size(axis)
    me = lax.axis_index(axis)
    bit = 1
    while bit < size:
        incoming = swapped(value, axis, bit)
        upper = (me // bit) % 2 == 1
        value = jnp.where(
            upper,
            jnp.concatenate([incoming, value], along),
            jnp.concatenate([value, incoming], along),
        )
        bit *= 2
    return value


def scatter_halving(value, axis):
    size = lax.axis_size(axis)
    me = lax.axis_index(axis)
    bit = size // 2
    while bit >= 1:
        half = value.shape[0] // 2
        low, high = value[:half], value[half:]
        upper = (me // bit) % 2 == 1
        send = jnp.where(upper, low, high)
        keep = jnp.where(upper, high, low)
        incoming = swapped(send.astype(jnp.bfloat16), axis, bit)
        value = keep + incoming.astype(jnp.float32)
        bit //= 2
    return value


def reduce_in_halves(value, axis):
    size = lax.axis_size(axis)
    me = lax.axis_index(axis)
    top = size // 2
    half = value.shape[0] // 2
    upper = (me // top) % 2 == 1
    send = jnp.where(upper, value[:half], value[half:])
    keep = jnp.where(upper, value[half:], value[:half])
    part = keep + swapped(send.astype(jnp.bfloat16), axis, top).astype(jnp.float32)
    bit = 1
    while bit < top:
        part = part + swapped(part.astype(jnp.bfloat16), axis, bit).astype(jnp.float32)
        bit *= 2
    part = part.astype(jnp.bfloat16)
    other = swapped(part, axis, top)
    return jnp.where(
        upper, jnp.concatenate([other, part], 0), jnp.concatenate([part, other], 0)
    )


def columns(value, head, depth):
    return value[:, head * depth : (head + 1) * depth]


def trans_dot(left, right):
    return lax.dot_general(left, right, (((1,), (1,)), ((), ())), preferred_element_type=jnp.float32)


def window_probs(queries, keys_all, marks_query, marks_all, depth, scale, block_rows):
    row_index = lax.broadcasted_iota(jnp.int32, (block_rows, block_rows + WINDOW), 0)
    col_index = lax.broadcasted_iota(jnp.int32, (block_rows, block_rows + WINDOW), 1)
    same_doc = marks_query[:, None] == marks_all[None, :]
    allowed = same_doc & (col_index > row_index) & (col_index <= row_index + WINDOW)
    result = []
    for head in range(queries.shape[1] // depth):
        scores = trans_dot(columns(queries, head, depth), columns(keys_all, head, depth)) * scale
        highest = jnp.max(jnp.where(allowed, scores, negative), axis=-1, keepdims=True)
        weights = jnp.where(allowed, jnp.exp(scores - highest), 0.0)
        totals = jnp.sum(weights, axis=-1, keepdims=True)
        result.append(weights / totals)
    return result


def mix_values(probability, values_all, depth):
    rounded = [part.astype(jnp.bfloat16) for part in probability]
    mixed = [
        jnp.dot(part, columns(values_all, head, depth), preferred_element_type=jnp.float32)
        for head, part in enumerate(rounded)
    ]
    return jnp.concatenate(mixed, 1).astype(jnp.bfloat16), rounded


def shards(
    teacher_query,
    teacher_key,
    teacher_value,
    student_query,
    student_key,
    student_value,
    segment_ids,
    language_ids,
    language_weight,
    teacher_out_proj,
    student_out_proj,
    match_proj,
):
    rows = teacher_query.shape[0]
    width = teacher_key.shape[1]
    reach = WINDOW // rows
    steps = reach // 2
    heads_t = teacher_query.shape[1] // DH_T
    heads_s = student_query.shape[1] // DH_S
    student_scale = DH_S ** (-0.5)
    doc_marks = segment_ids + 1
    mark_rows = jnp.pad(doc_marks.astype(jnp.bfloat16), (0, 8 * width - rows)).reshape(8, width)
    own = jnp.concatenate([teacher_key, teacher_value, student_key, student_value, mark_rows], 0)
    chain = [own]
    for _ in range(steps):
        chain.append(shifted(chain[-1], "seq", 2))
    core = lax.axis_index("seq") % 2
    stacked = jnp.stack(chain)
    partner = swapped(lax.dynamic_slice_in_dim(stacked, core, steps, 0), "seq", 1)
    pieces = []
    for k in range(steps, 0, -1):
        pieces.append(chain[k])
        pieces.append(partner[k - 1])
    pieces.append(own)
    window = jnp.stack(pieces)
    span = window.shape[0] * rows
    keys_teacher = window[:, 0:rows].reshape(span, width)
    values_teacher = window[:, rows : 2 * rows].reshape(span, width)
    keys_student = window[:, 2 * rows : 3 * rows].reshape(span, width)
    values_student = window[:, 3 * rows : 4 * rows].reshape(span, width)
    marks_all = (
        window[:, 4 * rows :].reshape(window.shape[0], 8 * width)[:, :rows].reshape(span)
    ).astype(jnp.int32)

    probability = window_probs(
        teacher_query, keys_teacher, doc_marks, marks_all, DH_T, teacher_scale, rows
    )
    teacher_mix, _ = mix_values(probability, values_teacher, DH_T)
    target_cols = lax.dot_general(
        gather_doubling(teacher_mix, "head", 1),
        teacher_out_proj,
        (((1,), (1,)), ((), ())),
        preferred_element_type=jnp.float32,
    ).astype(jnp.bfloat16)

    probability = window_probs(
        student_query, keys_student, doc_marks, marks_all, DH_S, student_scale, rows
    )
    student_mix, rounded = mix_values(probability, values_student, DH_S)
    lang_table = lax.broadcasted_iota(jnp.int32, (rows, language_weight.shape[0]), 1)
    token_weight = jnp.sum(
        jnp.where(language_ids[:, None] == lang_table, language_weight[None, :], 0.0), axis=1
    )
    weighted = token_weight[:, None] * (
        jnp.dot(student_mix, student_out_proj, preferred_element_type=jnp.float32)
        - jnp.dot(target_cols, match_proj, preferred_element_type=jnp.float32)
    )
    grad_mix = reduce_in_halves(weighted, "head")
    grad_heads = lax.dot_general(
        grad_mix,
        student_out_proj,
        (((1,), (1,)), ((), ())),
        preferred_element_type=jnp.float32,
    ).astype(jnp.bfloat16)

    grad_q, grad_k, grad_v = [], [], []
    for head, (part, low) in enumerate(zip(probability, rounded)):
        grad_here = columns(grad_heads, head, DH_S)
        grad_probs = trans_dot(grad_here, columns(values_student, head, DH_S))
        inner = jnp.sum(part * grad_probs, axis=-1, keepdims=True)
        grad_scores = (part * (grad_probs - inner)).astype(jnp.bfloat16)
        grad_q.append(
            student_scale
            * jnp.dot(grad_scores, columns(keys_student, head, DH_S), preferred_element_type=jnp.float32)
        )
        grad_k.append(
            student_scale
            * jnp.dot(grad_scores.T, columns(student_query, head, DH_S), preferred_element_type=jnp.float32)
        )
        grad_v.append(jnp.dot(low.T, grad_here, preferred_element_type=jnp.float32))
    grad_q = jnp.concatenate(grad_q, 1)
    grad_k = jnp.concatenate(grad_k, 1)
    grad_v = jnp.concatenate(grad_v, 1)
    blocks = span // rows
    grads = jnp.concatenate(
        [grad_k.reshape(blocks, rows, width), grad_v.reshape(blocks, rows, width)], 1
    )
    from_partner = swapped(grads[1::2], "seq", 1)
    nothing = jnp.zeros_like(from_partner[:1])
    added = jnp.where(
        core == 1,
        jnp.concatenate([from_partner, nothing], 0),
        jnp.concatenate([nothing, from_partner], 0),
    )
    even = grads[0::2] + added
    total = even[0]
    for k in range(1, steps + 1):
        total = even[k] + shifted(total.astype(jnp.bfloat16), "seq", -2).astype(jnp.float32)
    return (grad_q, total[:rows], total[rows:])


def solution(mesh):
    in_specs = (
        P("seq", "head"),
        P("seq", "head"),
        P("seq", "head"),
        P("seq", "head"),
        P("seq", "head"),
        P("seq", "head"),
        P("seq"),
        P("seq"),
        P(),
        P("head", None),
        P("head", None),
        P("head", None),
    )
    out_specs = (P("seq", "head"), P("seq", "head"), P("seq", "head"))
    return jax.shard_map(shards, mesh=mesh, in_specs=in_specs, out_specs=out_specs, check_vma=False)
```

```python
import jax
import jax.numpy as jnp
from jax import lax
from jax.sharding import PartitionSpec as P

DH_T = 128
DH_S = 256
WINDOW = 1024


teacher_scale = 144.0 ** (-0.5)
negative = -1e30


def shifted(value, axis, by):
    length = lax.axis_size(axis)
    pairs = [(i, i + by) for i in range(length) if 0 <= i + by < length]
    return lax.ppermute(value, axis, pairs)


def swapped(value, axis, bit):
    length = lax.axis_size(axis)
    return lax.ppermute(value, axis, [(i, i ^ bit) for i in range(length)])


def gather_doubling(value, axis, along):
    size = lax.axis_size(axis)
    me = lax.axis_index(axis)
    bit = 1
    while bit < size:
        incoming = swapped(value, axis, bit)
        upper = (me // bit) % 2 == 1
        value = jnp.where(
            upper,
            jnp.concatenate([incoming, value], along),
            jnp.concatenate([value, incoming], along),
        )
        bit *= 2
    return value


def scatter_halving(value, axis):
    size = lax.axis_size(axis)
    me = lax.axis_index(axis)
    bit = size // 2
    while bit >= 1:
        half = value.shape[0] // 2
        low, high = value[:half], value[half:]
        upper = (me // bit) % 2 == 1
        send = jnp.where(upper, low, high)
        keep = jnp.where(upper, high, low)
        incoming = swapped(send.astype(jnp.bfloat16), axis, bit)
        value = keep + incoming.astype(jnp.float32)
        bit //= 2
    return value


def reduce_in_halves(value, axis):
    size = lax.axis_size(axis)
    me = lax.axis_index(axis)
    top = size // 2
    half = value.shape[0] // 2
    upper = (me // top) % 2 == 1
    send = jnp.where(upper, value[:half], value[half:])
    keep = jnp.where(upper, value[half:], value[:half])
    part = keep + swapped(send.astype(jnp.bfloat16), axis, top).astype(jnp.float32)
    bit = 1
    while bit < top:
        part = part + swapped(part.astype(jnp.bfloat16), axis, bit).astype(jnp.float32)
        bit *= 2
    part = part.astype(jnp.bfloat16)
    other = swapped(part, axis, top)
    return jnp.where(
        upper, jnp.concatenate([other, part], 0), jnp.concatenate([part, other], 0)
    )


def columns(value, head, depth):
    return value[:, head * depth : (head + 1) * depth]


def trans_dot(left, right):
    return lax.dot_general(left, right, (((1,), (1,)), ((), ())), preferred_element_type=jnp.float32)


def window_probs(queries, keys_all, marks_query, marks_all, depth, scale, block_rows):
    row_index = lax.broadcasted_iota(jnp.int32, (block_rows, block_rows + WINDOW), 0)
    col_index = lax.broadcasted_iota(jnp.int32, (block_rows, block_rows + WINDOW), 1)
    same_doc = marks_query[:, None] == marks_all[None, :]
    allowed = same_doc & (col_index > row_index) & (col_index <= row_index + WINDOW)
    result = []
    for head in range(queries.shape[1] // depth):
        scores = trans_dot(columns(queries, head, depth), columns(keys_all, head, depth)) * scale
        highest = jnp.max(jnp.where(allowed, scores, negative), axis=-1, keepdims=True)
        weights = jnp.where(allowed, jnp.exp(scores - highest), 0.0)
        totals = jnp.sum(weights, axis=-1, keepdims=True)
        result.append(weights / totals)
    return result


def mix_values(probability, values_all, depth):
    rounded = [part.astype(jnp.bfloat16) for part in probability]
    mixed = [
        jnp.dot(part, columns(values_all, head, depth), preferred_element_type=jnp.float32)
        for head, part in enumerate(rounded)
    ]
    return jnp.concatenate(mixed, 1).astype(jnp.bfloat16), rounded


def shards(
    teacher_query,
    teacher_key,
    teacher_value,
    student_query,
    student_key,
    student_value,
    segment_ids,
    language_ids,
    language_weight,
    teacher_out_proj,
    student_out_proj,
    match_proj,
):
    rows = teacher_query.shape[0]
    width = teacher_key.shape[1]
    reach = WINDOW // rows
    steps = reach // 2
    heads_t = teacher_query.shape[1] // DH_T
    heads_s = student_query.shape[1] // DH_S
    student_scale = DH_S ** (-0.5)
    doc_marks = segment_ids + 1
    mark_rows = jnp.pad(doc_marks.astype(jnp.bfloat16), (0, 8 * width - rows)).reshape(8, width)
    own = jnp.concatenate([teacher_key, teacher_value, student_key, student_value, mark_rows], 0)
    core = lax.axis_index("seq") % 2
    chain = [own]
    partner = []
    pending = None
    for _ in range(steps):
        step = shifted(chain[-1], "seq", 2)
        if pending is not None:
            step, pending = lax.optimization_barrier((step, pending))
            partner.append(pending)
        chain.append(step)
        pending = swapped(jnp.where(core == 0, chain[-2], chain[-1]), "seq", 1)
    partner.append(pending)
    pieces = []
    for k in range(steps, 0, -1):
        pieces.append(chain[k])
        pieces.append(partner[k - 1])
    pieces.append(own)
    window = jnp.stack(pieces)
    span = window.shape[0] * rows
    keys_teacher = window[:, 0:rows].reshape(span, width)
    values_teacher = window[:, rows : 2 * rows].reshape(span, width)
    keys_student = window[:, 2 * rows : 3 * rows].reshape(span, width)
    values_student = window[:, 3 * rows : 4 * rows].reshape(span, width)
    marks_all = (
        window[:, 4 * rows :].reshape(window.shape[0], 8 * width)[:, :rows].reshape(span)
    ).astype(jnp.int32)

    probability = window_probs(
        teacher_query, keys_teacher, doc_marks, marks_all, DH_T, teacher_scale, rows
    )
    teacher_mix, _ = mix_values(probability, values_teacher, DH_T)
    target_cols = lax.dot_general(
        gather_doubling(teacher_mix, "head", 1),
        teacher_out_proj,
        (((1,), (1,)), ((), ())),
        preferred_element_type=jnp.float32,
    ).astype(jnp.bfloat16)

    probability = window_probs(
        student_query, keys_student, doc_marks, marks_all, DH_S, student_scale, rows
    )
    student_mix, rounded = mix_values(probability, values_student, DH_S)
    lang_table = lax.broadcasted_iota(jnp.int32, (rows, language_weight.shape[0]), 1)
    token_weight = jnp.sum(
        jnp.where(language_ids[:, None] == lang_table, language_weight[None, :], 0.0), axis=1
    )
    weighted = token_weight[:, None] * (
        jnp.dot(student_mix, student_out_proj, preferred_element_type=jnp.float32)
        - jnp.dot(target_cols, match_proj, preferred_element_type=jnp.float32)
    )
    grad_mix = reduce_in_halves(weighted, "head")
    grad_heads = lax.dot_general(
        grad_mix,
        student_out_proj,
        (((1,), (1,)), ((), ())),
        preferred_element_type=jnp.float32,
    ).astype(jnp.bfloat16)

    grad_q, grad_k, grad_v = [], [], []
    for head, (part, low) in enumerate(zip(probability, rounded)):
        grad_here = columns(grad_heads, head, DH_S)
        grad_probs = trans_dot(grad_here, columns(values_student, head, DH_S))
        inner = jnp.sum(part * grad_probs, axis=-1, keepdims=True)
        grad_scores = (part * (grad_probs - inner)).astype(jnp.bfloat16)
        grad_q.append(
            student_scale
            * jnp.dot(grad_scores, columns(keys_student, head, DH_S), preferred_element_type=jnp.float32)
        )
        grad_k.append(
            student_scale
            * jnp.dot(grad_scores.T, columns(student_query, head, DH_S), preferred_element_type=jnp.float32)
        )
        grad_v.append(jnp.dot(low.T, grad_here, preferred_element_type=jnp.float32))
    grad_q = jnp.concatenate(grad_q, 1)
    grad_k = jnp.concatenate(grad_k, 1)
    grad_v = jnp.concatenate(grad_v, 1)
    blocks = span // rows
    grads = jnp.concatenate(
        [grad_k.reshape(blocks, rows, width), grad_v.reshape(blocks, rows, width)], 1
    )
    from_partner = swapped(grads[1::2].astype(jnp.bfloat16), "seq", 1).astype(jnp.float32)
    nothing = jnp.zeros_like(from_partner[:1])
    added = jnp.where(
        core == 1,
        jnp.concatenate([from_partner, nothing], 0),
        jnp.concatenate([nothing, from_partner], 0),
    )
    even = grads[0::2] + added
    total = even[0]
    for k in range(1, steps + 1):
        total = even[k] + shifted(total.astype(jnp.bfloat16), "seq", -2).astype(jnp.float32)
    return (grad_q, total[:rows], total[rows:])


def solution(mesh):
    in_specs = (
        P("seq", "head"),
        P("seq", "head"),
        P("seq", "head"),
        P("seq", "head"),
        P("seq", "head"),
        P("seq", "head"),
        P("seq"),
        P("seq"),
        P(),
        P("head", None),
        P("head", None),
        P("head", None),
    )
    out_specs = (P("seq", "head"), P("seq", "head"), P("seq", "head"))
    return jax.shard_map(shards, mesh=mesh, in_specs=in_specs, out_specs=out_specs, check_vma=False)
```

```python
import jax
import jax.numpy as jnp
from jax import lax
from jax.sharding import PartitionSpec as P

DH_T = 128
DH_S = 256
WINDOW = 1024


teacher_scale = 144.0 ** (-0.5)
negative = -1e30


def shifted(value, axis, by):
    length = lax.axis_size(axis)
    pairs = [(i, i + by) for i in range(length) if 0 <= i + by < length]
    return lax.ppermute(value, axis, pairs)


def swapped(value, axis, bit):
    length = lax.axis_size(axis)
    return lax.ppermute(value, axis, [(i, i ^ bit) for i in range(length)])


def gather_doubling(value, axis, along):
    size = lax.axis_size(axis)
    me = lax.axis_index(axis)
    bit = 1
    while bit < size:
        incoming = swapped(value, axis, bit)
        upper = (me // bit) % 2 == 1
        value = jnp.where(
            upper,
            jnp.concatenate([incoming, value], along),
            jnp.concatenate([value, incoming], along),
        )
        bit *= 2
    return value


def scatter_halving(value, axis):
    size = lax.axis_size(axis)
    me = lax.axis_index(axis)
    bit = size // 2
    while bit >= 1:
        half = value.shape[0] // 2
        low, high = value[:half], value[half:]
        upper = (me // bit) % 2 == 1
        send = jnp.where(upper, low, high)
        keep = jnp.where(upper, high, low)
        incoming = swapped(send.astype(jnp.bfloat16), axis, bit)
        value = keep + incoming.astype(jnp.float32)
        bit //= 2
    return value


def reduce_in_halves(value, axis):
    size = lax.axis_size(axis)
    me = lax.axis_index(axis)
    top = size // 2
    half = value.shape[0] // 2
    upper = (me // top) % 2 == 1
    send = jnp.where(upper, value[:half], value[half:])
    keep = jnp.where(upper, value[half:], value[:half])
    part = keep + swapped(send.astype(jnp.bfloat16), axis, top).astype(jnp.float32)
    bit = 1
    while bit < top:
        part = part + swapped(part.astype(jnp.bfloat16), axis, bit).astype(jnp.float32)
        bit *= 2
    part = part.astype(jnp.bfloat16)
    other = swapped(part, axis, top)
    return jnp.where(
        upper, jnp.concatenate([other, part], 0), jnp.concatenate([part, other], 0)
    )


def columns(value, head, depth):
    return value[:, head * depth : (head + 1) * depth]


def trans_dot(left, right):
    return lax.dot_general(left, right, (((1,), (1,)), ((), ())), preferred_element_type=jnp.float32)


def window_probs(queries, keys_all, marks_query, marks_all, depth, scale, block_rows):
    row_index = lax.broadcasted_iota(jnp.int32, (block_rows, block_rows + WINDOW), 0)
    col_index = lax.broadcasted_iota(jnp.int32, (block_rows, block_rows + WINDOW), 1)
    same_doc = marks_query[:, None] == marks_all[None, :]
    allowed = same_doc & (col_index > row_index) & (col_index <= row_index + WINDOW)
    result = []
    for head in range(queries.shape[1] // depth):
        scores = trans_dot(columns(queries, head, depth), columns(keys_all, head, depth)) * scale
        highest = jnp.max(jnp.where(allowed, scores, negative), axis=-1, keepdims=True)
        weights = jnp.where(allowed, jnp.exp(scores - highest), 0.0)
        totals = jnp.sum(weights, axis=-1, keepdims=True)
        result.append(weights / totals)
    return result


def mix_values(probability, values_all, depth):
    rounded = [part.astype(jnp.bfloat16) for part in probability]
    mixed = [
        jnp.dot(part, columns(values_all, head, depth), preferred_element_type=jnp.float32)
        for head, part in enumerate(rounded)
    ]
    return jnp.concatenate(mixed, 1).astype(jnp.bfloat16), rounded


def project_while_gathering(value, weight, axis):
    size = lax.axis_size(axis)
    me = lax.axis_index(axis)
    block = value.shape[1]

    def product(part, first, count):
        cols = lax.dynamic_slice_in_dim(weight, first * block, count * block, 1)
        return trans_dot(part, cols)

    total = product(value, me, 1)
    held = value
    bit = 1
    while bit < size:
        incoming = swapped(held, axis, bit)
        total = total + product(incoming, ((me ^ bit) // bit) * bit, bit)
        upper = (me // bit) % 2 == 1
        held = jnp.where(
            upper,
            jnp.concatenate([incoming, held], 1),
            jnp.concatenate([held, incoming], 1),
        )
        bit *= 2
    return total


def shards(
    teacher_query,
    teacher_key,
    teacher_value,
    student_query,
    student_key,
    student_value,
    segment_ids,
    language_ids,
    language_weight,
    teacher_out_proj,
    student_out_proj,
    match_proj,
):
    rows = teacher_query.shape[0]
    width = teacher_key.shape[1]
    reach = WINDOW // rows
    steps = reach // 2
    heads_t = teacher_query.shape[1] // DH_T
    heads_s = student_query.shape[1] // DH_S
    student_scale = DH_S ** (-0.5)
    doc_marks = segment_ids + 1
    mark_rows = jnp.pad(doc_marks.astype(jnp.bfloat16), (0, 8 * width - rows)).reshape(8, width)
    own = jnp.concatenate([teacher_key, teacher_value, student_key, student_value, mark_rows], 0)
    chain = [own]
    for _ in range(steps):
        chain.append(shifted(chain[-1], "seq", 2))
    core = lax.axis_index("seq") % 2
    stacked = jnp.stack(chain)
    partner = swapped(lax.dynamic_slice_in_dim(stacked, core, steps, 0), "seq", 1)
    pieces = []
    for k in range(steps, 0, -1):
        pieces.append(chain[k])
        pieces.append(partner[k - 1])
    pieces.append(own)
    window = jnp.stack(pieces)
    span = window.shape[0] * rows
    keys_teacher = window[:, 0:rows].reshape(span, width)
    values_teacher = window[:, rows : 2 * rows].reshape(span, width)
    keys_student = window[:, 2 * rows : 3 * rows].reshape(span, width)
    values_student = window[:, 3 * rows : 4 * rows].reshape(span, width)
    marks_all = (
        window[:, 4 * rows :].reshape(window.shape[0], 8 * width)[:, :rows].reshape(span)
    ).astype(jnp.int32)

    probability = window_probs(
        teacher_query, keys_teacher, doc_marks, marks_all, DH_T, teacher_scale, rows
    )
    teacher_mix, _ = mix_values(probability, values_teacher, DH_T)
    target_cols = project_while_gathering(teacher_mix, teacher_out_proj, "head").astype(
        jnp.bfloat16
    )

    probability = window_probs(
        student_query, keys_student, doc_marks, marks_all, DH_S, student_scale, rows
    )
    student_mix, rounded = mix_values(probability, values_student, DH_S)
    lang_table = lax.broadcasted_iota(jnp.int32, (rows, language_weight.shape[0]), 1)
    token_weight = jnp.sum(
        jnp.where(language_ids[:, None] == lang_table, language_weight[None, :], 0.0), axis=1
    )
    weighted = token_weight[:, None] * (
        jnp.dot(student_mix, student_out_proj, preferred_element_type=jnp.float32)
        - jnp.dot(target_cols, match_proj, preferred_element_type=jnp.float32)
    )
    grad_mix = reduce_in_halves(weighted, "head")
    grad_heads = lax.dot_general(
        grad_mix,
        student_out_proj,
        (((1,), (1,)), ((), ())),
        preferred_element_type=jnp.float32,
    ).astype(jnp.bfloat16)

    grad_q, grad_k, grad_v = [], [], []
    for head, (part, low) in enumerate(zip(probability, rounded)):
        grad_here = columns(grad_heads, head, DH_S)
        grad_probs = trans_dot(grad_here, columns(values_student, head, DH_S))
        inner = jnp.sum(part * grad_probs, axis=-1, keepdims=True)
        grad_scores = (part * (grad_probs - inner)).astype(jnp.bfloat16)
        grad_q.append(
            student_scale
            * jnp.dot(grad_scores, columns(keys_student, head, DH_S), preferred_element_type=jnp.float32)
        )
        grad_k.append(
            student_scale
            * jnp.dot(grad_scores.T, columns(student_query, head, DH_S), preferred_element_type=jnp.float32)
        )
        grad_v.append(jnp.dot(low.T, grad_here, preferred_element_type=jnp.float32))
    grad_q = jnp.concatenate(grad_q, 1)
    grad_k = jnp.concatenate(grad_k, 1)
    grad_v = jnp.concatenate(grad_v, 1)
    blocks = span // rows
    grads = jnp.concatenate(
        [grad_k.reshape(blocks, rows, width), grad_v.reshape(blocks, rows, width)], 1
    )
    from_partner = swapped(grads[1::2].astype(jnp.bfloat16), "seq", 1).astype(jnp.float32)
    nothing = jnp.zeros_like(from_partner[:1])
    added = jnp.where(
        core == 1,
        jnp.concatenate([from_partner, nothing], 0),
        jnp.concatenate([nothing, from_partner], 0),
    )
    even = grads[0::2] + added
    total = even[0]
    for k in range(1, steps + 1):
        total = even[k] + shifted(total.astype(jnp.bfloat16), "seq", -2).astype(jnp.float32)
    return (grad_q, total[:rows], total[rows:])


def solution(mesh):
    in_specs = (
        P("seq", "head"),
        P("seq", "head"),
        P("seq", "head"),
        P("seq", "head"),
        P("seq", "head"),
        P("seq", "head"),
        P("seq"),
        P("seq"),
        P(),
        P("head", None),
        P("head", None),
        P("head", None),
    )
    out_specs = (P("seq", "head"), P("seq", "head"), P("seq", "head"))
    return jax.shard_map(shards, mesh=mesh, in_specs=in_specs, out_specs=out_specs, check_vma=False)
```

```python
import jax
import jax.numpy as jnp
from jax import lax
from jax.sharding import PartitionSpec as P

DH_T = 128
DH_S = 256
WINDOW = 1024


teacher_scale = 144.0 ** (-0.5)
negative = -1e30


def shifted(value, axis, by):
    length = lax.axis_size(axis)
    pairs = [(i, i + by) for i in range(length) if 0 <= i + by < length]
    return lax.ppermute(value, axis, pairs)


def swapped(value, axis, bit):
    length = lax.axis_size(axis)
    return lax.ppermute(value, axis, [(i, i ^ bit) for i in range(length)])


def gather_doubling(value, axis, along):
    size = lax.axis_size(axis)
    me = lax.axis_index(axis)
    bit = 1
    while bit < size:
        incoming = swapped(value, axis, bit)
        upper = (me // bit) % 2 == 1
        value = jnp.where(
            upper,
            jnp.concatenate([incoming, value], along),
            jnp.concatenate([value, incoming], along),
        )
        bit *= 2
    return value


def scatter_halving(value, axis):
    size = lax.axis_size(axis)
    me = lax.axis_index(axis)
    bit = size // 2
    while bit >= 1:
        half = value.shape[0] // 2
        low, high = value[:half], value[half:]
        upper = (me // bit) % 2 == 1
        send = jnp.where(upper, low, high)
        keep = jnp.where(upper, high, low)
        incoming = swapped(send.astype(jnp.bfloat16), axis, bit)
        value = keep + incoming.astype(jnp.float32)
        bit //= 2
    return value


def reduce_in_halves(value, axis):
    size = lax.axis_size(axis)
    me = lax.axis_index(axis)
    top = size // 2
    half = value.shape[0] // 2
    upper = (me // top) % 2 == 1
    send = jnp.where(upper, value[:half], value[half:])
    keep = jnp.where(upper, value[half:], value[:half])
    part = keep + swapped(send.astype(jnp.bfloat16), axis, top).astype(jnp.float32)
    bit = 1
    while bit < top:
        part = part + swapped(part.astype(jnp.bfloat16), axis, bit).astype(jnp.float32)
        bit *= 2
    part = part.astype(jnp.bfloat16)
    other = swapped(part, axis, top)
    return jnp.where(
        upper, jnp.concatenate([other, part], 0), jnp.concatenate([part, other], 0)
    )


def columns(value, head, depth):
    return value[:, head * depth : (head + 1) * depth]


def trans_dot(left, right):
    return lax.dot_general(left, right, (((1,), (1,)), ((), ())), preferred_element_type=jnp.float32)


def window_probs(queries, keys_all, marks_query, marks_all, depth, scale, block_rows):
    row_index = lax.broadcasted_iota(jnp.int32, (block_rows, block_rows + WINDOW), 0)
    col_index = lax.broadcasted_iota(jnp.int32, (block_rows, block_rows + WINDOW), 1)
    same_doc = marks_query[:, None] == marks_all[None, :]
    allowed = same_doc & (col_index > row_index) & (col_index <= row_index + WINDOW)
    result = []
    for head in range(queries.shape[1] // depth):
        scores = trans_dot(columns(queries, head, depth), columns(keys_all, head, depth)) * scale
        highest = jnp.max(jnp.where(allowed, scores, negative), axis=-1, keepdims=True)
        weights = jnp.where(allowed, jnp.exp(scores - highest), 0.0)
        totals = jnp.sum(weights, axis=-1, keepdims=True)
        result.append(weights / totals)
    return result


def mix_values(probability, values_all, depth):
    rounded = [part.astype(jnp.bfloat16) for part in probability]
    mixed = [
        jnp.dot(part, columns(values_all, head, depth), preferred_element_type=jnp.float32)
        for head, part in enumerate(rounded)
    ]
    return jnp.concatenate(mixed, 1).astype(jnp.bfloat16), rounded


def shards(
    teacher_query,
    teacher_key,
    teacher_value,
    student_query,
    student_key,
    student_value,
    segment_ids,
    language_ids,
    language_weight,
    teacher_out_proj,
    student_out_proj,
    match_proj,
):
    rows = teacher_query.shape[0]
    width = teacher_key.shape[1]
    reach = WINDOW // rows
    steps = reach // 2
    heads_t = teacher_query.shape[1] // DH_T
    heads_s = student_query.shape[1] // DH_S
    student_scale = DH_S ** (-0.5)
    doc_marks = segment_ids + 1
    mark_rows = jnp.pad(doc_marks.astype(jnp.bfloat16), (0, 8 * width - rows)).reshape(8, width)
    own = jnp.concatenate([teacher_key, teacher_value, student_key, student_value, mark_rows], 0)
    chain = [own]
    for _ in range(steps):
        chain.append(shifted(chain[-1], "seq", 2))
    core = lax.axis_index("seq") % 2
    stacked = jnp.stack(chain)
    partner = swapped(lax.dynamic_slice_in_dim(stacked, core, steps, 0), "seq", 1)
    pieces = []
    for k in range(steps, 0, -1):
        pieces.append(chain[k])
        pieces.append(partner[k - 1])
    pieces.append(own)
    window = jnp.stack(pieces)
    span = window.shape[0] * rows
    keys_teacher = window[:, 0:rows].reshape(span, width)
    values_teacher = window[:, rows : 2 * rows].reshape(span, width)
    keys_student = window[:, 2 * rows : 3 * rows].reshape(span, width)
    values_student = window[:, 3 * rows : 4 * rows].reshape(span, width)
    marks_all = (
        window[:, 4 * rows :].reshape(window.shape[0], 8 * width)[:, :rows].reshape(span)
    ).astype(jnp.int32)

    probability = window_probs(
        teacher_query, keys_teacher, doc_marks, marks_all, DH_T, teacher_scale, rows
    )
    teacher_mix, _ = mix_values(probability, values_teacher, DH_T)
    target_cols = lax.dot_general(
        gather_doubling(teacher_mix, "head", 1),
        teacher_out_proj,
        (((1,), (1,)), ((), ())),
        preferred_element_type=jnp.float32,
    ).astype(jnp.bfloat16)

    probability = window_probs(
        student_query, keys_student, doc_marks, marks_all, DH_S, student_scale, rows
    )
    student_mix, rounded = mix_values(probability, values_student, DH_S)
    lang_table = lax.broadcasted_iota(jnp.int32, (rows, language_weight.shape[0]), 1)
    token_weight = jnp.sum(
        jnp.where(language_ids[:, None] == lang_table, language_weight[None, :], 0.0), axis=1
    )
    weighted = token_weight[:, None] * (
        jnp.dot(student_mix, student_out_proj, preferred_element_type=jnp.float32)
        - jnp.dot(target_cols, match_proj, preferred_element_type=jnp.float32)
    )
    grad_mix = reduce_in_halves(weighted, "head")
    grad_heads = lax.dot_general(
        grad_mix,
        student_out_proj,
        (((1,), (1,)), ((), ())),
        preferred_element_type=jnp.float32,
    ).astype(jnp.bfloat16)

    grad_q, grad_k, grad_v = [], [], []
    for head, (part, low) in enumerate(zip(probability, rounded)):
        grad_here = columns(grad_heads, head, DH_S)
        grad_probs = trans_dot(grad_here, columns(values_student, head, DH_S))
        inner = jnp.sum(part * grad_probs, axis=-1, keepdims=True)
        grad_scores = (part * (grad_probs - inner)).astype(jnp.bfloat16)
        grad_q.append(
            student_scale
            * jnp.dot(grad_scores, columns(keys_student, head, DH_S), preferred_element_type=jnp.float32)
        )
        grad_k.append(
            student_scale
            * jnp.dot(grad_scores.T, columns(student_query, head, DH_S), preferred_element_type=jnp.float32)
        )
        grad_v.append(jnp.dot(low.T, grad_here, preferred_element_type=jnp.float32))
    grad_q = jnp.concatenate(grad_q, 1)
    grad_k = jnp.concatenate(grad_k, 1)
    grad_v = jnp.concatenate(grad_v, 1)
    blocks = span // rows
    grads = jnp.concatenate(
        [grad_k.reshape(blocks, rows, width), grad_v.reshape(blocks, rows, width)], 1
    )
    from_partner = swapped(grads[1::2].astype(jnp.bfloat16), "seq", 1).astype(jnp.float32)
    nothing = jnp.zeros_like(from_partner[:1])
    added = jnp.where(
        core == 1,
        jnp.concatenate([from_partner, nothing], 0),
        jnp.concatenate([nothing, from_partner], 0),
    )
    even = grads[0::2] + added
    total = even[0]
    for k in range(1, steps + 1):
        total = even[k] + shifted(total.astype(jnp.bfloat16), "seq", -2).astype(jnp.float32)
    return (grad_q, total[:rows], total[rows:])


def solution(mesh):
    in_specs = (
        P("seq", "head"),
        P("seq", "head"),
        P("seq", "head"),
        P("seq", "head"),
        P("seq", "head"),
        P("seq", "head"),
        P("seq"),
        P("seq"),
        P(),
        P("head", None),
        P("head", None),
        P("head", None),
    )
    out_specs = (P("seq", "head"), P("seq", "head"), P("seq", "head"))
    return jax.shard_map(shards, mesh=mesh, in_specs=in_specs, out_specs=out_specs, check_vma=False)
```

```python
import jax
import jax.numpy as jnp
from jax import lax
from jax.sharding import PartitionSpec as P

DH_T = 128
DH_S = 256
WINDOW = 1024


teacher_scale = 144.0 ** (-0.5)
negative = -1e30


def shifted(value, axis, by):
    length = lax.axis_size(axis)
    pairs = [(i, i + by) for i in range(length) if 0 <= i + by < length]
    return lax.ppermute(value, axis, pairs)


def swapped(value, axis, bit):
    length = lax.axis_size(axis)
    return lax.ppermute(value, axis, [(i, i ^ bit) for i in range(length)])


def gather_doubling(value, axis, along):
    size = lax.axis_size(axis)
    me = lax.axis_index(axis)
    bit = 1
    while bit < size:
        incoming = swapped(value, axis, bit)
        upper = (me // bit) % 2 == 1
        value = jnp.where(
            upper,
            jnp.concatenate([incoming, value], along),
            jnp.concatenate([value, incoming], along),
        )
        bit *= 2
    return value


def scatter_halving(value, axis):
    size = lax.axis_size(axis)
    me = lax.axis_index(axis)
    bit = size // 2
    while bit >= 1:
        half = value.shape[0] // 2
        low, high = value[:half], value[half:]
        upper = (me // bit) % 2 == 1
        send = jnp.where(upper, low, high)
        keep = jnp.where(upper, high, low)
        incoming = swapped(send.astype(jnp.bfloat16), axis, bit)
        value = keep + incoming.astype(jnp.float32)
        bit //= 2
    return value


def reduce_in_halves(value, axis):
    size = lax.axis_size(axis)
    me = lax.axis_index(axis)
    top = size // 2
    half = value.shape[0] // 2
    upper = (me // top) % 2 == 1
    send = jnp.where(upper, value[:half], value[half:])
    keep = jnp.where(upper, value[half:], value[:half])
    part = keep + swapped(send.astype(jnp.bfloat16), axis, top).astype(jnp.float32)
    bit = 1
    while bit < top:
        part = part + swapped(part.astype(jnp.bfloat16), axis, bit).astype(jnp.float32)
        bit *= 2
    part = part.astype(jnp.bfloat16)
    other = swapped(part, axis, top)
    return jnp.where(
        upper, jnp.concatenate([other, part], 0), jnp.concatenate([part, other], 0)
    )


def columns(value, head, depth):
    return value[:, head * depth : (head + 1) * depth]


def trans_dot(left, right):
    return lax.dot_general(left, right, (((1,), (1,)), ((), ())), preferred_element_type=jnp.float32)


def window_probs(queries, keys_all, marks_query, marks_all, depth, scale, block_rows):
    row_index = lax.broadcasted_iota(jnp.int32, (block_rows, block_rows + WINDOW), 0)
    col_index = lax.broadcasted_iota(jnp.int32, (block_rows, block_rows + WINDOW), 1)
    same_doc = marks_query[:, None] == marks_all[None, :]
    allowed = same_doc & (col_index > row_index) & (col_index <= row_index + WINDOW)
    result = []
    for head in range(queries.shape[1] // depth):
        scores = trans_dot(columns(queries, head, depth), columns(keys_all, head, depth)) * scale
        highest = jnp.max(jnp.where(allowed, scores, negative), axis=-1, keepdims=True)
        weights = jnp.where(allowed, jnp.exp(scores - highest), 0.0)
        totals = jnp.sum(weights, axis=-1, keepdims=True)
        result.append(weights / totals)
    return result


def mix_values(probability, values_all, depth):
    rounded = [part.astype(jnp.bfloat16) for part in probability]
    mixed = [
        jnp.dot(part, columns(values_all, head, depth), preferred_element_type=jnp.float32)
        for head, part in enumerate(rounded)
    ]
    return jnp.concatenate(mixed, 1).astype(jnp.bfloat16), rounded


def shards(
    teacher_query,
    teacher_key,
    teacher_value,
    student_query,
    student_key,
    student_value,
    segment_ids,
    language_ids,
    language_weight,
    teacher_out_proj,
    student_out_proj,
    match_proj,
):
    rows = teacher_query.shape[0]
    width = teacher_key.shape[1]
    reach = WINDOW // rows
    steps = reach // 2
    heads_t = teacher_query.shape[1] // DH_T
    heads_s = student_query.shape[1] // DH_S
    student_scale = DH_S ** (-0.5)
    doc_marks = segment_ids + 1
    mark_rows = jnp.pad(doc_marks.astype(jnp.bfloat16), (0, 8 * width - rows)).reshape(8, width)
    own = jnp.concatenate([teacher_key, teacher_value, student_key, student_value, mark_rows], 0)
    chain = [own]
    for _ in range(steps):
        chain.append(shifted(chain[-1], "seq", 2))
    core = lax.axis_index("seq") % 2
    stacked = jnp.stack(chain)
    partner = swapped(lax.dynamic_slice_in_dim(stacked, core, steps, 0), "seq", 1)
    pieces = []
    for k in range(steps, 0, -1):
        pieces.append(chain[k])
        pieces.append(partner[k - 1])
    pieces.append(own)
    window = jnp.stack(pieces)
    span = window.shape[0] * rows
    keys_teacher = window[:, 0:rows].reshape(span, width)
    values_teacher = window[:, rows : 2 * rows].reshape(span, width)
    keys_student = window[:, 2 * rows : 3 * rows].reshape(span, width)
    values_student = window[:, 3 * rows : 4 * rows].reshape(span, width)
    marks_all = (
        window[:, 4 * rows :].reshape(window.shape[0], 8 * width)[:, :rows].reshape(span)
    ).astype(jnp.int32)

    probability = window_probs(
        teacher_query, keys_teacher, doc_marks, marks_all, DH_T, teacher_scale, rows
    )
    teacher_mix, _ = mix_values(probability, values_teacher, DH_T)
    target_cols = lax.dot_general(
        gather_doubling(teacher_mix, "head", 1),
        teacher_out_proj,
        (((1,), (1,)), ((), ())),
        preferred_element_type=jnp.float32,
    ).astype(jnp.bfloat16)

    probability = window_probs(
        student_query, keys_student, doc_marks, marks_all, DH_S, student_scale, rows
    )
    student_mix, rounded = mix_values(probability, values_student, DH_S)
    lang_table = lax.broadcasted_iota(jnp.int32, (rows, language_weight.shape[0]), 1)
    token_weight = jnp.sum(
        jnp.where(language_ids[:, None] == lang_table, language_weight[None, :], 0.0), axis=1
    )
    weighted = token_weight[:, None] * (
        jnp.dot(student_mix, student_out_proj, preferred_element_type=jnp.float32)
        - jnp.dot(target_cols, match_proj, preferred_element_type=jnp.float32)
    )
    grad_mix = reduce_in_halves(weighted, "head")
    grad_heads = lax.dot_general(
        grad_mix,
        student_out_proj,
        (((1,), (1,)), ((), ())),
        preferred_element_type=jnp.float32,
    ).astype(jnp.bfloat16)

    grad_q, grad_k, grad_v = [], [], []
    for head, (part, low) in enumerate(zip(probability, rounded)):
        grad_here = columns(grad_heads, head, DH_S)
        grad_probs = trans_dot(grad_here, columns(values_student, head, DH_S))
        inner = jnp.sum(part * grad_probs, axis=-1, keepdims=True)
        grad_scores = (part * (grad_probs - inner)).astype(jnp.bfloat16)
        grad_q.append(
            student_scale
            * jnp.dot(grad_scores, columns(keys_student, head, DH_S), preferred_element_type=jnp.float32)
        )
        grad_k.append(
            student_scale
            * jnp.dot(grad_scores.T, columns(student_query, head, DH_S), preferred_element_type=jnp.float32)
        )
        grad_v.append(jnp.dot(low.T, grad_here, preferred_element_type=jnp.float32))
    grad_q = jnp.concatenate(grad_q, 1)
    grad_k = jnp.concatenate(grad_k, 1)
    grad_v = jnp.concatenate(grad_v, 1)
    blocks = span // rows
    grads = jnp.concatenate(
        [grad_k.reshape(blocks, rows, width), grad_v.reshape(blocks, rows, width)], 1
    )
    from_partner = swapped(grads[1::2].astype(jnp.bfloat16), "seq", 1).astype(jnp.float32)
    nothing = jnp.zeros_like(from_partner[0])
    evens = steps + 1

    def even(k):
        after = from_partner[k] if k < evens - 1 else nothing
        before = from_partner[k - 1] if k > 0 else nothing
        return grads[2 * k] + jnp.where(core == 1, after, before)

    total = even(0)
    for k in range(1, evens):
        total = even(k) + shifted(total.astype(jnp.bfloat16), "seq", -2).astype(jnp.float32)
    return (grad_q, total[:rows], total[rows:])


def solution(mesh):
    in_specs = (
        P("seq", "head"),
        P("seq", "head"),
        P("seq", "head"),
        P("seq", "head"),
        P("seq", "head"),
        P("seq", "head"),
        P("seq"),
        P("seq"),
        P(),
        P("head", None),
        P("head", None),
        P("head", None),
    )
    out_specs = (P("seq", "head"), P("seq", "head"), P("seq", "head"))
    return jax.shard_map(shards, mesh=mesh, in_specs=in_specs, out_specs=out_specs, check_vma=False)
```

```python
import jax
import jax.numpy as jnp
from jax import lax
from jax.sharding import PartitionSpec as P

DH_T = 128
DH_S = 256
WINDOW = 1024


teacher_scale = 144.0 ** (-0.5)
negative = -1e30


def shifted(value, axis, by):
    length = lax.axis_size(axis)
    pairs = [(i, i + by) for i in range(length) if 0 <= i + by < length]
    return lax.ppermute(value, axis, pairs)


def swapped(value, axis, bit):
    length = lax.axis_size(axis)
    return lax.ppermute(value, axis, [(i, i ^ bit) for i in range(length)])


def gather_doubling(value, axis, along):
    size = lax.axis_size(axis)
    me = lax.axis_index(axis)
    bit = 1
    while bit < size:
        incoming = swapped(value, axis, bit)
        upper = (me // bit) % 2 == 1
        value = jnp.where(
            upper,
            jnp.concatenate([incoming, value], along),
            jnp.concatenate([value, incoming], along),
        )
        bit *= 2
    return value


def scatter_halving(value, axis):
    size = lax.axis_size(axis)
    me = lax.axis_index(axis)
    bit = size // 2
    while bit >= 1:
        half = value.shape[0] // 2
        low, high = value[:half], value[half:]
        upper = (me // bit) % 2 == 1
        send = jnp.where(upper, low, high)
        keep = jnp.where(upper, high, low)
        incoming = swapped(send.astype(jnp.bfloat16), axis, bit)
        value = keep + incoming.astype(jnp.float32)
        bit //= 2
    return value


def reduce_in_halves(value, axis):
    size = lax.axis_size(axis)
    me = lax.axis_index(axis)
    top = size // 2
    half = value.shape[0] // 2
    upper = (me // top) % 2 == 1
    send = jnp.where(upper, value[:half], value[half:])
    keep = jnp.where(upper, value[half:], value[:half])
    part = keep + swapped(send.astype(jnp.bfloat16), axis, top).astype(jnp.float32)
    bit = 1
    while bit < top:
        part = part + swapped(part.astype(jnp.bfloat16), axis, bit).astype(jnp.float32)
        bit *= 2
    part = part.astype(jnp.bfloat16)
    other = swapped(part, axis, top)
    return jnp.where(
        upper, jnp.concatenate([other, part], 0), jnp.concatenate([part, other], 0)
    )


def columns(value, head, depth):
    return value[:, head * depth : (head + 1) * depth]


def trans_dot(left, right):
    return lax.dot_general(left, right, (((1,), (1,)), ((), ())), preferred_element_type=jnp.float32)


def window_probs(queries, keys_all, marks_query, marks_all, depth, scale, block_rows):
    row_index = lax.broadcasted_iota(jnp.int32, (block_rows, block_rows + WINDOW), 0)
    col_index = lax.broadcasted_iota(jnp.int32, (block_rows, block_rows + WINDOW), 1)
    same_doc = marks_query[:, None] == marks_all[None, :]
    allowed = same_doc & (col_index > row_index) & (col_index <= row_index + WINDOW)
    result = []
    for head in range(queries.shape[1] // depth):
        scores = trans_dot(columns(queries, head, depth), columns(keys_all, head, depth)) * scale
        highest = jnp.max(jnp.where(allowed, scores, negative), axis=-1, keepdims=True)
        weights = jnp.where(allowed, jnp.exp(scores - highest), 0.0)
        totals = jnp.sum(weights, axis=-1, keepdims=True)
        result.append(weights / totals)
    return result


def mix_values(probability, values_all, depth):
    rounded = [part.astype(jnp.bfloat16) for part in probability]
    mixed = [
        jnp.dot(part, columns(values_all, head, depth), preferred_element_type=jnp.float32)
        for head, part in enumerate(rounded)
    ]
    return jnp.concatenate(mixed, 1).astype(jnp.bfloat16), rounded


def shards(
    teacher_query,
    teacher_key,
    teacher_value,
    student_query,
    student_key,
    student_value,
    segment_ids,
    language_ids,
    language_weight,
    teacher_out_proj,
    student_out_proj,
    match_proj,
):
    rows = teacher_query.shape[0]
    width = teacher_key.shape[1]
    reach = WINDOW // rows
    steps = reach // 2
    heads_t = teacher_query.shape[1] // DH_T
    heads_s = student_query.shape[1] // DH_S
    student_scale = DH_S ** (-0.5)
    doc_marks = segment_ids + 1
    mark_rows = jnp.pad(doc_marks.astype(jnp.bfloat16), (0, 8 * width - rows)).reshape(8, width)
    own = jnp.concatenate(
        [jnp.stack([teacher_key, teacher_value, student_key, student_value]).reshape(4 * rows, width), mark_rows],
        0,
    )
    chain = [own]
    for _ in range(steps):
        chain.append(shifted(chain[-1], "seq", 2))
    core = lax.axis_index("seq") % 2
    stacked = jnp.stack(chain)
    partner = swapped(lax.dynamic_slice_in_dim(stacked, core, steps, 0), "seq", 1)
    pieces = []
    for k in range(steps, 0, -1):
        pieces.append(chain[k])
        pieces.append(partner[k - 1])
    pieces.append(own)
    window = jnp.stack(pieces)
    span = window.shape[0] * rows
    keys_teacher = window[:, 0:rows].reshape(span, width)
    values_teacher = window[:, rows : 2 * rows].reshape(span, width)
    keys_student = window[:, 2 * rows : 3 * rows].reshape(span, width)
    values_student = window[:, 3 * rows : 4 * rows].reshape(span, width)
    marks_all = (
        window[:, 4 * rows :].reshape(window.shape[0], 8 * width)[:, :rows].reshape(span)
    ).astype(jnp.int32)

    probability = window_probs(
        teacher_query, keys_teacher, doc_marks, marks_all, DH_T, teacher_scale, rows
    )
    teacher_mix, _ = mix_values(probability, values_teacher, DH_T)
    target_cols = lax.dot_general(
        gather_doubling(teacher_mix, "head", 1),
        teacher_out_proj,
        (((1,), (1,)), ((), ())),
        preferred_element_type=jnp.float32,
    ).astype(jnp.bfloat16)

    probability = window_probs(
        student_query, keys_student, doc_marks, marks_all, DH_S, student_scale, rows
    )
    student_mix, rounded = mix_values(probability, values_student, DH_S)
    lang_table = lax.broadcasted_iota(jnp.int32, (rows, language_weight.shape[0]), 1)
    token_weight = jnp.sum(
        jnp.where(language_ids[:, None] == lang_table, language_weight[None, :], 0.0), axis=1
    )
    weighted = token_weight[:, None] * (
        jnp.dot(student_mix, student_out_proj, preferred_element_type=jnp.float32)
        - jnp.dot(target_cols, match_proj, preferred_element_type=jnp.float32)
    )
    grad_mix = reduce_in_halves(weighted, "head")
    grad_heads = lax.dot_general(
        grad_mix,
        student_out_proj,
        (((1,), (1,)), ((), ())),
        preferred_element_type=jnp.float32,
    ).astype(jnp.bfloat16)

    grad_q, grad_k, grad_v = [], [], []
    for head, (part, low) in enumerate(zip(probability, rounded)):
        grad_here = columns(grad_heads, head, DH_S)
        grad_probs = trans_dot(grad_here, columns(values_student, head, DH_S))
        inner = jnp.sum(part * grad_probs, axis=-1, keepdims=True)
        grad_scores = (part * (grad_probs - inner)).astype(jnp.bfloat16)
        grad_q.append(
            student_scale
            * jnp.dot(grad_scores, columns(keys_student, head, DH_S), preferred_element_type=jnp.float32)
        )
        grad_k.append(
            student_scale
            * jnp.dot(grad_scores.T, columns(student_query, head, DH_S), preferred_element_type=jnp.float32)
        )
        grad_v.append(jnp.dot(low.T, grad_here, preferred_element_type=jnp.float32))
    grad_q = jnp.concatenate(grad_q, 1)
    grad_k = jnp.concatenate(grad_k, 1)
    grad_v = jnp.concatenate(grad_v, 1)
    blocks = span // rows
    grads = jnp.concatenate(
        [grad_k.reshape(blocks, rows, width), grad_v.reshape(blocks, rows, width)], 1
    )
    from_partner = swapped(grads[1::2].astype(jnp.bfloat16), "seq", 1).astype(jnp.float32)
    nothing = jnp.zeros_like(from_partner[:1])
    added = jnp.where(
        core == 1,
        jnp.concatenate([from_partner, nothing], 0),
        jnp.concatenate([nothing, from_partner], 0),
    )
    even = grads[0::2] + added
    total = even[0]
    for k in range(1, steps + 1):
        total = even[k] + shifted(total.astype(jnp.bfloat16), "seq", -2).astype(jnp.float32)
    return (grad_q, total[:rows], total[rows:])


def solution(mesh):
    in_specs = (
        P("seq", "head"),
        P("seq", "head"),
        P("seq", "head"),
        P("seq", "head"),
        P("seq", "head"),
        P("seq", "head"),
        P("seq"),
        P("seq"),
        P(),
        P("head", None),
        P("head", None),
        P("head", None),
    )
    out_specs = (P("seq", "head"), P("seq", "head"), P("seq", "head"))
    return jax.shard_map(shards, mesh=mesh, in_specs=in_specs, out_specs=out_specs, check_vma=False)
```
